128 devices in a mesh: dp: 16 (over z, y_lo, core), land: 8 (over x, y_hi).
Axes of the slice: x: 4, y: 4 (y_hi: 2, y_lo: 2; y = y_hi * 2 + y_lo), z: 4, core: 2. Of those that a mesh axis runs over, the one named last changes fastest.
Arguments:
- doc_values: bfloat16 [24576, 1024], P('dp'), may hold values from 0 to 100
- doc_blocks: int32 [192, 8], P('dp'), may hold values from 0 to 511, as said below
- land_values: bfloat16 [16384, 1024], P(('dp', 'land')), may hold values from 0 to 100
- land_blocks: int32 [128, 8], replicated, may hold values from 0 to 511, as said below
- coefficients: bfloat16 [16384, 64], P(('dp', 'land')), may hold values from -12 to 12
Outputs:
- normal_product: float32 [16384, 64], P(('dp', 'land'))
The draws below stay inside these ranges and needn't reach their ends.
Inputs may be any that keep to these rules, and one draw needn't show every extreme that they name: `doc_blocks`: each row lists 8 different vocabulary block numbers. `land_blocks`: each row lists 8 different vocabulary block numbers.
All inputs are finite; a program needn't handle non-finite values.
Results may differ from the reference program's by a relative error of at most 0.0003.
Values may be sent and summed in bfloat16 or wider, within the bound.
No kernel may reach another device: no remote copies, remote signals or barrier semaphores. Data moves between devices by JAX's collectives and lax.ppermute only.
A program may use at most 64 MiB of HBM per device.

```python
import math
import jax
import jax.numpy as jnp
from jax import lax

VOCAB_BLOCKS = 512
TERM_BLOCK = 128
ACTIVE = 8
LAND_ACTIVE = 8
DOC_BLOCK = 128
LM_BLOCK = 128
TARGETS = 64
LANDMARKS = 16384
DOCS = 24576


topic_count = 4


def block_lists(key, salt, rows, picks):
    popular = jax.random.permutation(jax.random.fold_in(key, 11), VOCAB_BLOCKS).astype(jnp.int32)
    numbers = jnp.arange(VOCAB_BLOCKS, dtype=jnp.int32)
    common = (numbers == 0) | (numbers == VOCAB_BLOCKS - 1)
    popular = jnp.where(common, VOCAB_BLOCKS + 64, popular).astype(jnp.int32)
    noise = jax.random.randint(jax.random.fold_in(key, salt), (rows, VOCAB_BLOCKS), 0, 1024)
    scores = (popular[None, :] * 32 + noise) * VOCAB_BLOCKS + numbers[None, :]
    _, chosen = jax.lax.top_k(scores, picks)
    return chosen.astype(jnp.int32)


def block_profiles(key):
    base = jax.random.fold_in(key, 41)
    shape = (VOCAB_BLOCKS, TERM_BLOCK)
    owner = jax.random.randint(jax.random.fold_in(base, 1), shape, 0, topic_count).astype(jnp.int32)
    present = jax.random.uniform(jax.random.fold_in(base, 2), shape) < 0.6
    levels = jnp.exp(jax.random.uniform(jax.random.fold_in(base, 3), shape, minval=math.log(0.1), maxval=0.0))
    idf = jnp.exp(jax.random.uniform(jax.random.fold_in(base, 4), shape, minval=0.0, maxval=math.log(10.0)))
    numbers = jnp.arange(VOCAB_BLOCKS, dtype=jnp.int32)
    common = (numbers == 0) | (numbers == VOCAB_BLOCKS - 1)
    block_scale = jnp.where(common, 3.0, 1.0).astype(jnp.float32)
    weight = idf * block_scale[:, None]
    profile = jnp.where(present, levels, 0.0) * weight
    return (owner, profile.astype(jnp.float32), weight.astype(jnp.float32))


def term_values(key, salt, lists, row_block):
    block_total = lists.shape[0]
    picks = lists.shape[1]
    width = picks * TERM_BLOCK
    rows = block_total * row_block
    owner, profile, weight = block_profiles(key)
    owner_rows = owner[lists].reshape(block_total, 1, width)
    profile_rows = profile[lists].reshape(block_total, 1, width)
    weight_rows = weight[lists].reshape(block_total, 1, width)
    base = jax.random.fold_in(key, salt)
    exponent = 2.5 * jax.random.normal(jax.random.fold_in(base, 5), (block_total, row_block, topic_count))
    mixing = jnp.exp(exponent - jnp.max(exponent, axis=2, keepdims=True))
    selected = jnp.zeros((block_total, row_block, width), jnp.float32)
    for topic in range(topic_count):
        selected = selected + jnp.where(owner_rows == topic, mixing[:, :, topic:topic + 1], 0.0)
    speckle = jax.random.uniform(jax.random.fold_in(base, 6), (block_total, row_block, width)) < 0.3
    amount = jax.random.uniform(jax.random.fold_in(base, 7), (block_total, row_block, width), minval=0.0, maxval=0.4)
    noise = jnp.where(speckle, amount, 0.0) * weight_rows
    values = selected * profile_rows + noise
    values = jnp.minimum(values, 100.0).astype(jnp.float32)
    return values.reshape(rows, width).astype(jnp.bfloat16)


def draw_doc_blocks(key, part):
    return block_lists(key, 13, DOCS // DOC_BLOCK, ACTIVE)


def draw_land_blocks(key, part):
    return block_lists(key, 17, LANDMARKS // LM_BLOCK, LAND_ACTIVE)


def draw_doc_values(key, part):
    lists = block_lists(key, 13, DOCS // DOC_BLOCK, ACTIVE)
    return term_values(key, 101, lists, DOC_BLOCK)


def draw_land_values(key, part):
    lists = block_lists(key, 17, LANDMARKS // LM_BLOCK, LAND_ACTIVE)
    return term_values(key, 202, lists, LM_BLOCK)


def steps_of(own_key, extent, pieces, low, top_value):
    gain = 1.0
    for position, parts in pieces:
        steps = jax.random.uniform(jax.random.fold_in(jax.random.fold_in(own_key, 6), position), (parts,), jnp.float32, low / len(pieces), top_value / len(pieces))
        gain = gain * jnp.repeat(jnp.exp(steps), extent[position] // parts).reshape((-1,) + (1,) * (len(extent) - 1 - position))
    return gain


def centred(own_key, dims, scale, most, pieces=(), held_as=jnp.bfloat16):
    loudness = steps_of(own_key, dims, pieces, -0.22, 0.18) if pieces else 1.0
    values = jax.random.normal(own_key, dims, jnp.float32) * scale * loudness
    return jnp.minimum(jnp.maximum(values, -most), most).astype(held_as)


def setup_inputs(seed: int = 0) -> dict:
    streams_of = jax.random.split(jax.random.key(seed), 6)
    return {
        "doc_values": draw_doc_values(jax.random.fold_in(streams_of[5], 71), 0),
        "doc_blocks": draw_doc_blocks(jax.random.fold_in(streams_of[5], 71), 0),
        "land_values": draw_land_values(jax.random.fold_in(streams_of[5], 71), 0),
        "land_blocks": draw_land_blocks(jax.random.fold_in(streams_of[5], 71), 0),
        "coefficients": centred(streams_of[4], (LANDMARKS, TARGETS), 2.0, 12.0, ((0, 128),)),
    }


sharpness = 2.0

def kernel_block(doc_grid, doc_blocks, doc_norm, tile_grid, tile_ids, tile_norms):
    matches = (doc_blocks[:, :, None] == tile_ids[None, None, :]).astype(jnp.float32)
    aligned = jnp.einsum('dab,lbt->dlat', matches, tile_grid.astype(jnp.float32)).astype(jnp.bfloat16)
    aligned = aligned.reshape(matches.shape[0], LM_BLOCK, ACTIVE * TERM_BLOCK)
    inner_terms = jnp.einsum('drw,dlw->drl', doc_grid.astype(jnp.float32), aligned.astype(jnp.float32))
    inner_terms = inner_terms.reshape(-1, LM_BLOCK)
    cosine = inner_terms * doc_norm[:, None] * tile_norms[None, :]
    kernel = jnp.exp(2.0 * sharpness * (cosine - 1.0))
    high = lax.optimization_barrier(kernel.astype(jnp.bfloat16))
    low = (kernel - high.astype(jnp.float32)).astype(jnp.bfloat16)
    return (high, low)

def reference(doc_values, doc_blocks, land_values, land_blocks, coefficients):
    doc_norm = lax.rsqrt(lax.optimization_barrier(jnp.sum(jnp.square(doc_values.astype(jnp.float32)), axis=1)) + 1e-06)
    land_norm = lax.rsqrt(lax.optimization_barrier(jnp.sum(jnp.square(land_values.astype(jnp.float32)), axis=1)) + 1e-06)
    doc_count = doc_values.shape[0] // DOC_BLOCK
    doc_grid = doc_values.reshape(doc_count, DOC_BLOCK, ACTIVE * TERM_BLOCK)
    land_count = LANDMARKS // LM_BLOCK
    land_grid = land_values.reshape(land_count, LM_BLOCK, LAND_ACTIVE, TERM_BLOCK)
    norm_grid = land_norm.reshape(land_count, LM_BLOCK)
    coef = coefficients.reshape(land_count, LM_BLOCK, TARGETS)

    def fit_block(running, packed):
        tile_grid, tile_ids, tile_norms, block_coef = packed
        high, low = kernel_block(doc_grid, doc_blocks, doc_norm, tile_grid, tile_ids, tile_norms)
        running = running + jnp.dot(high, block_coef, preferred_element_type=jnp.float32)
        running = running + jnp.dot(low, block_coef, preferred_element_type=jnp.float32)
        return (running, None)
    fitted, _ = lax.scan(fit_block, jnp.zeros((DOCS, TARGETS), jnp.float32), (land_grid, land_blocks, norm_grid, coef))
    fitted_high = lax.optimization_barrier(fitted.astype(jnp.bfloat16))
    fitted_low = (fitted - fitted_high.astype(jnp.float32)).astype(jnp.bfloat16)
    fitted_pair = jnp.concatenate([fitted_high, fitted_low], axis=1)

    def back_block(packed):
        tile_grid, tile_ids, tile_norms = packed
        high, low = kernel_block(doc_grid, doc_blocks, doc_norm, tile_grid, tile_ids, tile_norms)
        summed = jnp.dot(high.T, fitted_pair, preferred_element_type=jnp.float32)
        summed = summed + jnp.dot(low.T, fitted_pair, preferred_element_type=jnp.float32)
        return (summed[:, :TARGETS] + summed[:, TARGETS:]) / DOCS
    result = lax.map(back_block, (land_grid, land_blocks, norm_grid))
    return result.reshape(LANDMARKS, TARGETS)
```

```python
import jax
import jax.numpy as jnp
from jax import lax
from jax.experimental import pallas as pl
from jax.experimental.pallas import tpu as pltpu
from jax.sharding import PartitionSpec as P

TERM_BLOCK = 128
ACTIVE = 8
LAND_ACTIVE = 8
DOC_BLOCK = 128
LM_BLOCK = 128


sharpness = 2.0


def split_pair(values):
    high = lax.optimization_barrier(values.astype(jnp.bfloat16))
    low = (values - high.astype(jnp.float32)).astype(jnp.bfloat16)
    return (high, low)


def match_table(doc_blocks, land_ids):
    eq = doc_blocks[None, :, :, None] == land_ids[:, None, None, :]
    has = jnp.any(eq, axis=2)
    first = jnp.argmax(eq, axis=2).astype(jnp.int32)
    return jnp.where(has, first, ACTIVE).astype(jnp.int32).reshape(-1)


def forward_kernel(slot_ref, doc_ref, dn_ref, land_ref, ln_ref, coef_ref,
                   high_ref, low_ref, fit_ref, aligned_ref):
    step = pl.program_id(0)
    doc_count = dn_ref.shape[0] // DOC_BLOCK

    @pl.when(step == 0)
    def _():
        fit_ref[...] = jnp.zeros_like(fit_ref)

    for d in range(doc_count):
        for b in range(LAND_ACTIVE):
            a = slot_ref[(step * doc_count + d) * LAND_ACTIVE + b]
            aligned_ref[d * DOC_BLOCK:(d + 1) * DOC_BLOCK, b * TERM_BLOCK:(b + 1) * TERM_BLOCK] = (
                doc_ref[d * (ACTIVE + 1) + a])
    inner = lax.dot_general(
        aligned_ref[...], land_ref[...], (((1,), (1,)), ((), ())),
        preferred_element_type=jnp.float32)
    cosine = inner * dn_ref[...] * ln_ref[0]
    kern = jnp.exp(2.0 * sharpness * (cosine - 1.0))
    high = kern.astype(jnp.bfloat16)
    low = (kern - high.astype(jnp.float32)).astype(jnp.bfloat16)
    high_ref[...] = high
    low_ref[...] = low
    coef = coef_ref[...]
    part = jnp.dot(high, coef, preferred_element_type=jnp.float32)
    part = part + jnp.dot(low, coef, preferred_element_type=jnp.float32)
    fit_ref[...] += part


def forward(slots, doc_tiles, doc_norm, land_rows, land_norm, coef_rows):
    doc_rows = doc_norm.shape[0]
    land_count = land_rows.shape[0]
    block_count = land_count // LM_BLOCK
    width = land_rows.shape[1]
    targets = coef_rows.shape[1]
    grid_spec = pltpu.PrefetchScalarGridSpec(
        num_scalar_prefetch=1,
        grid=(block_count,),
        in_specs=[
            pl.BlockSpec(doc_tiles.shape, lambda l, s: (0, 0, 0)),
            pl.BlockSpec((doc_rows, 1), lambda l, s: (0, 0)),
            pl.BlockSpec((LM_BLOCK, width), lambda l, s: (l, 0)),
            pl.BlockSpec((1, 1, LM_BLOCK), lambda l, s: (l, 0, 0)),
            pl.BlockSpec((LM_BLOCK, targets), lambda l, s: (l, 0)),
        ],
        out_specs=[
            pl.BlockSpec((doc_rows, LM_BLOCK), lambda l, s: (0, l)),
            pl.BlockSpec((doc_rows, LM_BLOCK), lambda l, s: (0, l)),
            pl.BlockSpec((doc_rows, targets), lambda l, s: (0, 0)),
        ],
        scratch_shapes=[pltpu.VMEM((doc_rows, width), jnp.bfloat16)],
    )
    return pl.pallas_call(
        forward_kernel,
        grid_spec=grid_spec,
        out_shape=[
            jax.ShapeDtypeStruct((doc_rows, land_count), jnp.bfloat16),
            jax.ShapeDtypeStruct((doc_rows, land_count), jnp.bfloat16),
            jax.ShapeDtypeStruct((doc_rows, targets), jnp.float32),
        ],
        compiler_params=pltpu.CompilerParams(
            dimension_semantics=("arbitrary",), vmem_limit_bytes=48 * 1024 * 1024),
    )(slots, doc_tiles, doc_norm, land_rows, land_norm.reshape(block_count, 1, LM_BLOCK), coef_rows)


def on_device(doc_values, doc_blocks, land_values, land_blocks, coefficients):
    dp_count = lax.axis_size("dp")
    land_count = lax.axis_size("land")
    doc_rows = doc_values.shape[0]
    targets = coefficients.shape[1]
    total_docs = doc_rows * dp_count
    own_blocks = land_values.shape[0] // LM_BLOCK
    doc_count = doc_rows // DOC_BLOCK
    doc_norm = lax.rsqrt(jnp.sum(jnp.square(doc_values.astype(jnp.float32)), axis=1) + 1e-06)
    land_norm = lax.rsqrt(jnp.sum(jnp.square(land_values.astype(jnp.float32)), axis=1) + 1e-06)
    table = land_blocks.reshape(dp_count, land_count, own_blocks, LAND_ACTIVE)
    own_table = lax.dynamic_index_in_dim(table, lax.axis_index("land"), axis=1, keepdims=False)
    own_table = own_table.reshape(dp_count * own_blocks, LAND_ACTIVE)
    land_rows = lax.all_gather(land_values, "dp", axis=0, tiled=True)
    coef_rows = lax.all_gather(coefficients, "dp", axis=0, tiled=True)
    norm_rows = lax.all_gather(land_norm, "dp", axis=0, tiled=True)
    doc_tiles = doc_values.reshape(doc_count, DOC_BLOCK, ACTIVE, TERM_BLOCK).transpose(0, 2, 1, 3)
    doc_tiles = jnp.pad(doc_tiles, ((0, 0), (0, 1), (0, 0), (0, 0)))
    doc_tiles = doc_tiles.reshape(doc_count * (ACTIVE + 1), DOC_BLOCK, TERM_BLOCK)
    slots = match_table(doc_blocks, own_table)
    tile_high, tile_low, fitted = forward(
        slots, doc_tiles, doc_norm.reshape(doc_rows, 1), land_rows, norm_rows, coef_rows)
    fitted = lax.psum(fitted, "land")
    fitted_high, fitted_low = split_pair(fitted)
    fitted_pair = jnp.concatenate([fitted_high, fitted_low], axis=1)
    summed = jnp.dot(tile_high.T, fitted_pair, preferred_element_type=jnp.float32)
    summed = summed + jnp.dot(tile_low.T, fitted_pair, preferred_element_type=jnp.float32)
    summed = summed[:, :targets] + summed[:, targets:]
    result = lax.psum_scatter(summed, "dp", scatter_dimension=0, tiled=True)
    return result / total_docs


def solution(mesh):
    placed = (P("dp", None), P("dp", None), P(("dp", "land"), None), P(), P(("dp", "land"), None))
    return jax.shard_map(
        on_device, mesh=mesh, in_specs=placed, out_specs=P(("dp", "land"), None), check_vma=False
    )
```

```python
import jax
import jax.numpy as jnp
from jax import lax
from jax.experimental import pallas as pl
from jax.experimental.pallas import tpu as pltpu
from jax.sharding import PartitionSpec as P

TERM_BLOCK = 128
ACTIVE = 8
LAND_ACTIVE = 8
DOC_BLOCK = 128
LM_BLOCK = 128


sharpness = 2.0


def split_pair(values):
    high = lax.optimization_barrier(values.astype(jnp.bfloat16))
    low = (values - high.astype(jnp.float32)).astype(jnp.bfloat16)
    return (high, low)


def match_table(doc_blocks, land_ids):
    eq = doc_blocks[None, :, :, None] == land_ids[:, None, None, :]
    has = jnp.any(eq, axis=2)
    first = jnp.argmax(eq, axis=2).astype(jnp.int32)
    return jnp.where(has, first, ACTIVE).astype(jnp.int32).reshape(-1)


def forward_kernel(slot_ref, doc_ref, dn_ref, land_ref,
                   high_ref, low_ref, fit_ref, aligned_ref):
    step = pl.program_id(0)
    doc_count = dn_ref.shape[0] // DOC_BLOCK

    @pl.when(step == 0)
    def _():
        fit_ref[...] = jnp.zeros_like(fit_ref)

    for d in range(doc_count):
        for b in range(LAND_ACTIVE):
            a = slot_ref[(step * doc_count + d) * LAND_ACTIVE + b]
            aligned_ref[d * DOC_BLOCK:(d + 1) * DOC_BLOCK, b * TERM_BLOCK:(b + 1) * TERM_BLOCK] = (
                doc_ref[d * (ACTIVE + 1) + a])
    width = ACTIVE * TERM_BLOCK
    tile = land_ref[:, :width]
    squares = jnp.zeros((LM_BLOCK, TERM_BLOCK), jnp.float32)
    for b in range(LAND_ACTIVE):
        part = tile[:, b * TERM_BLOCK:(b + 1) * TERM_BLOCK].astype(jnp.float32)
        squares = squares + part * part
    land_norm = lax.rsqrt(jnp.sum(squares.T, axis=0, keepdims=True) + 1e-06)
    inner = lax.dot_general(
        aligned_ref[...], tile, (((1,), (1,)), ((), ())),
        preferred_element_type=jnp.float32)
    cosine = inner * dn_ref[...] * land_norm
    kern = jnp.exp(2.0 * sharpness * (cosine - 1.0))
    high = kern.astype(jnp.bfloat16)
    low = (kern - high.astype(jnp.float32)).astype(jnp.bfloat16)
    high_ref[...] = high
    low_ref[...] = low
    coef = land_ref[:, width:]
    part = jnp.dot(high, coef, preferred_element_type=jnp.float32)
    part = part + jnp.dot(low, coef, preferred_element_type=jnp.float32)
    fit_ref[...] += part


def forward(slots, doc_tiles, doc_norm, land_rows, targets):
    doc_rows = doc_norm.shape[0]
    land_count = land_rows.shape[0]
    block_count = land_count // LM_BLOCK
    width = ACTIVE * TERM_BLOCK
    grid_spec = pltpu.PrefetchScalarGridSpec(
        num_scalar_prefetch=1,
        grid=(block_count,),
        in_specs=[
            pl.BlockSpec(doc_tiles.shape, lambda l, s: (0, 0, 0)),
            pl.BlockSpec((doc_rows, 1), lambda l, s: (0, 0)),
            pl.BlockSpec((LM_BLOCK, land_rows.shape[1]), lambda l, s: (l, 0)),
        ],
        out_specs=[
            pl.BlockSpec((doc_rows, LM_BLOCK), lambda l, s: (0, l)),
            pl.BlockSpec((doc_rows, LM_BLOCK), lambda l, s: (0, l)),
            pl.BlockSpec((doc_rows, targets), lambda l, s: (0, 0)),
        ],
        scratch_shapes=[pltpu.VMEM((doc_rows, width), jnp.bfloat16)],
    )
    return pl.pallas_call(
        forward_kernel,
        grid_spec=grid_spec,
        out_shape=[
            jax.ShapeDtypeStruct((doc_rows, land_count), jnp.bfloat16),
            jax.ShapeDtypeStruct((doc_rows, land_count), jnp.bfloat16),
            jax.ShapeDtypeStruct((doc_rows, targets), jnp.float32),
        ],
        compiler_params=pltpu.CompilerParams(
            dimension_semantics=("arbitrary",), vmem_limit_bytes=48 * 1024 * 1024),
    )(slots, doc_tiles, doc_norm, land_rows)


def gather_rows(rows, dp_count):
    own = lax.axis_index("dp")
    parts = [rows]
    sources = [own]
    for k in range(1, dp_count // 2):
        shift = [(i, (i + 2 * k) % dp_count) for i in range(dp_count)]
        parts.append(lax.ppermute(rows, "dp", shift))
        sources.append((own - 2 * k) % dp_count)
    mine = jnp.concatenate(parts, axis=0)
    other = lax.ppermute(mine, "dp", [(i, i ^ 1) for i in range(dp_count)])
    sources = sources + [s ^ 1 for s in sources]
    return jnp.concatenate([mine, other], axis=0), jnp.stack(sources).astype(jnp.int32)


def sum_over(values, axis, count):
    pieces = values.reshape((count, values.shape[0] // count) + values.shape[1:])
    pieces = lax.all_to_all(pieces, axis, 0, 0, tiled=False)
    return jnp.sum(pieces, axis=0)


def all_sum(values, axis, count):
    mine = sum_over(values, axis, count)
    spread = jnp.broadcast_to(mine[None], (count,) + mine.shape)
    return lax.all_to_all(spread, axis, 0, 0, tiled=False).reshape(values.shape)


def on_device(doc_values, doc_blocks, land_values, land_blocks, coefficients):
    dp_count = lax.axis_size("dp")
    land_count = lax.axis_size("land")
    doc_rows = doc_values.shape[0]
    targets = coefficients.shape[1]
    total_docs = doc_rows * dp_count
    own_blocks = land_values.shape[0] // LM_BLOCK
    doc_count = doc_rows // DOC_BLOCK
    doc_norm = lax.rsqrt(jnp.sum(jnp.square(doc_values.astype(jnp.float32)), axis=1) + 1e-06)
    table = land_blocks.reshape(dp_count, land_count, own_blocks, LAND_ACTIVE)
    own_table = lax.dynamic_index_in_dim(table, lax.axis_index("land"), axis=1, keepdims=False)
    own_table = own_table.reshape(dp_count * own_blocks, LAND_ACTIVE)
    land_rows, sources = gather_rows(jnp.concatenate([land_values, coefficients], axis=1), dp_count)
    own_table = own_table[sources]
    doc_tiles = doc_values.reshape(doc_count, DOC_BLOCK, ACTIVE, TERM_BLOCK).transpose(0, 2, 1, 3)
    doc_tiles = jnp.pad(doc_tiles, ((0, 0), (0, 1), (0, 0), (0, 0)))
    doc_tiles = doc_tiles.reshape(doc_count * (ACTIVE + 1), DOC_BLOCK, TERM_BLOCK)
    slots = match_table(doc_blocks, own_table)
    tile_high, tile_low, fitted = forward(
        slots, doc_tiles, doc_norm.reshape(doc_rows, 1), land_rows, targets)
    fitted = all_sum(fitted, "land", land_count)
    fitted_high, fitted_low = split_pair(fitted)
    fitted_pair = jnp.concatenate([fitted_high, fitted_low], axis=1)
    summed = jnp.dot(tile_high.T, fitted_pair, preferred_element_type=jnp.float32)
    summed = summed + jnp.dot(tile_low.T, fitted_pair, preferred_element_type=jnp.float32)
    summed = summed[:, :targets] + summed[:, targets:]
    order = jnp.argsort(sources)
    summed = summed.reshape(dp_count, own_blocks * LM_BLOCK, targets)[order]
    result = sum_over(summed.reshape(-1, targets), "dp", dp_count)
    return result / total_docs


def solution(mesh):
    placed = (P("dp", None), P("dp", None), P(("dp", "land"), None), P(), P(("dp", "land"), None))
    return jax.shard_map(
        on_device, mesh=mesh, in_specs=placed, out_specs=P(("dp", "land"), None), check_vma=False
    )
```

```python
import jax
import jax.numpy as jnp
from jax import lax
from jax.experimental import pallas as pl
from jax.experimental.pallas import tpu as pltpu
from jax.sharding import PartitionSpec as P

TERM_BLOCK = 128
ACTIVE = 8
LAND_ACTIVE = 8
DOC_BLOCK = 128
LM_BLOCK = 128


sharpness = 2.0


def split_pair(values):
    high = lax.optimization_barrier(values.astype(jnp.bfloat16))
    low = (values - high.astype(jnp.float32)).astype(jnp.bfloat16)
    return (high, low)


def match_table(doc_blocks, land_ids):
    eq = doc_blocks[None, :, :, None] == land_ids[:, None, None, :]
    has = jnp.any(eq, axis=2)
    first = jnp.argmax(eq, axis=2).astype(jnp.int32)
    return jnp.where(has, first, ACTIVE).astype(jnp.int32).reshape(-1)


def forward_kernel(slot_ref, doc_ref, dn_ref, *rest):
    part_count = len(rest) - 6
    parts = rest[:part_count]
    high_ref, low_ref, fit_ref, buf_ref, sem_ref, aligned_ref = rest[part_count:]
    step = pl.program_id(0)
    doc_count = dn_ref.shape[0] // DOC_BLOCK
    slot = step % 2

    @pl.when(step == 0)
    def _():
        fit_ref[...] = jnp.zeros_like(fit_ref)
        pltpu.make_async_copy(parts[0], buf_ref.at[0], sem_ref.at[0]).start()

    for k in range(1, part_count):
        @pl.when(step + 1 == k)
        def _():
            pltpu.make_async_copy(parts[k], buf_ref.at[k % 2], sem_ref.at[k % 2]).start()

    for d in range(doc_count):
        for b in range(LAND_ACTIVE):
            a = slot_ref[(step * doc_count + d) * LAND_ACTIVE + b]
            aligned_ref[d * DOC_BLOCK:(d + 1) * DOC_BLOCK, b * TERM_BLOCK:(b + 1) * TERM_BLOCK] = (
                doc_ref[d * (ACTIVE + 1) + a])
    pltpu.make_async_copy(parts[0], buf_ref.at[slot], sem_ref.at[slot]).wait()
    width = ACTIVE * TERM_BLOCK
    block = buf_ref.at[slot]
    tile = block[:, :width]
    squares = jnp.zeros((LM_BLOCK, TERM_BLOCK), jnp.float32)
    for b in range(LAND_ACTIVE):
        part = tile[:, b * TERM_BLOCK:(b + 1) * TERM_BLOCK].astype(jnp.float32)
        squares = squares + part * part
    land_norm = lax.rsqrt(jnp.sum(squares.T, axis=0, keepdims=True) + 1e-06)
    inner = lax.dot_general(
        aligned_ref[...], tile, (((1,), (1,)), ((), ())),
        preferred_element_type=jnp.float32)
    cosine = inner * dn_ref[...] * land_norm
    kern = jnp.exp(2.0 * sharpness * (cosine - 1.0))
    high = kern.astype(jnp.bfloat16)
    low = (kern - high.astype(jnp.float32)).astype(jnp.bfloat16)
    high_ref[...] = high
    low_ref[...] = low
    coef = block[:, width:]
    part = jnp.dot(high, coef, preferred_element_type=jnp.float32)
    part = part + jnp.dot(low, coef, preferred_element_type=jnp.float32)
    fit_ref[...] += part


def forward(slots, doc_tiles, doc_norm, parts, targets):
    doc_rows = doc_norm.shape[0]
    part_count = len(parts)
    land_count = part_count * LM_BLOCK
    width = ACTIVE * TERM_BLOCK
    row_width = parts[0].shape[1]
    grid_spec = pltpu.PrefetchScalarGridSpec(
        num_scalar_prefetch=1,
        grid=(part_count,),
        in_specs=[
            pl.BlockSpec(doc_tiles.shape, lambda l, s: (0, 0, 0)),
            pl.BlockSpec((doc_rows, 1), lambda l, s: (0, 0)),
        ] + [pl.BlockSpec(memory_space=pl.ANY)] * part_count,
        out_specs=[
            pl.BlockSpec((doc_rows, LM_BLOCK), lambda l, s: (0, l)),
            pl.BlockSpec((doc_rows, LM_BLOCK), lambda l, s: (0, l)),
            pl.BlockSpec((doc_rows, targets), lambda l, s: (0, 0)),
        ],
        scratch_shapes=[
            pltpu.VMEM((2, LM_BLOCK, row_width), jnp.bfloat16),
            pltpu.SemaphoreType.DMA((2,)),
            pltpu.VMEM((doc_rows, width), jnp.bfloat16),
        ],
    )
    return pl.pallas_call(
        forward_kernel,
        grid_spec=grid_spec,
        out_shape=[
            jax.ShapeDtypeStruct((doc_rows, land_count), jnp.bfloat16),
            jax.ShapeDtypeStruct((doc_rows, land_count), jnp.bfloat16),
            jax.ShapeDtypeStruct((doc_rows, targets), jnp.float32),
        ],
        compiler_params=pltpu.CompilerParams(
            dimension_semantics=("arbitrary",), vmem_limit_bytes=48 * 1024 * 1024),
    )(slots, doc_tiles, doc_norm, *parts)


def gather_rows(rows, dp_count):
    own = lax.axis_index("dp")
    parts = [rows]
    sources = [own]
    for k in range(1, dp_count // 2):
        shift = [(i, (i + 2 * k) % dp_count) for i in range(dp_count)]
        parts.append(lax.ppermute(rows, "dp", shift))
        sources.append((own - 2 * k) % dp_count)
    partner = [(i, i ^ 1) for i in range(dp_count)]
    others = [lax.ppermute(p, "dp", partner) for p in parts]
    sources = sources + [s ^ 1 for s in sources]
    return parts, others, jnp.stack(sources).astype(jnp.int32)


def sum_over(values, axis, count):
    pieces = values.reshape((count, values.shape[0] // count) + values.shape[1:])
    pieces = lax.all_to_all(pieces, axis, 0, 0, tiled=False)
    return jnp.sum(pieces, axis=0)


def all_sum(values, axis, count):
    mine = sum_over(values, axis, count)
    spread = jnp.broadcast_to(mine[None], (count,) + mine.shape)
    return lax.all_to_all(spread, axis, 0, 0, tiled=False).reshape(values.shape)


def on_device(doc_values, doc_blocks, land_values, land_blocks, coefficients):
    dp_count = lax.axis_size("dp")
    land_count = lax.axis_size("land")
    doc_rows = doc_values.shape[0]
    targets = coefficients.shape[1]
    total_docs = doc_rows * dp_count
    own_blocks = land_values.shape[0] // LM_BLOCK
    doc_count = doc_rows // DOC_BLOCK
    doc_norm = lax.rsqrt(jnp.sum(jnp.square(doc_values.astype(jnp.float32)), axis=1) + 1e-06)
    table = land_blocks.reshape(dp_count, land_count, own_blocks, LAND_ACTIVE)
    own_table = lax.dynamic_index_in_dim(table, lax.axis_index("land"), axis=1, keepdims=False)
    own_table = own_table.reshape(dp_count * own_blocks, LAND_ACTIVE)
    parts, others, sources = gather_rows(jnp.concatenate([land_values, coefficients], axis=1), dp_count)
    own_table = own_table[sources]
    half = len(parts)
    doc_tiles = doc_values.reshape(doc_count, DOC_BLOCK, ACTIVE, TERM_BLOCK).transpose(0, 2, 1, 3)
    doc_tiles = jnp.pad(doc_tiles, ((0, 0), (0, 1), (0, 0), (0, 0)))
    doc_tiles = doc_tiles.reshape(doc_count * (ACTIVE + 1), DOC_BLOCK, TERM_BLOCK)
    doc_norm = doc_norm.reshape(doc_rows, 1)
    high_one, low_one, fitted_one = forward(
        match_table(doc_blocks, own_table[:half]), doc_tiles, doc_norm, parts, targets)
    high_two, low_two, fitted_two = forward(
        match_table(doc_blocks, own_table[half:]), doc_tiles, doc_norm, others, targets)
    fitted = all_sum(fitted_one + fitted_two, "land", land_count)
    fitted_high, fitted_low = split_pair(fitted)
    fitted_pair = jnp.concatenate([fitted_high, fitted_low], axis=1)
    summed = []
    for tile_high, tile_low in ((high_one, low_one), (high_two, low_two)):
        part = jnp.dot(tile_high.T, fitted_pair, preferred_element_type=jnp.float32)
        part = part + jnp.dot(tile_low.T, fitted_pair, preferred_element_type=jnp.float32)
        summed.append(part[:, :targets] + part[:, targets:])
    summed = jnp.concatenate(summed, axis=0)
    order = jnp.argsort(sources)
    summed = summed.reshape(dp_count, own_blocks * LM_BLOCK, targets)[order]
    result = sum_over(summed.reshape(-1, targets), "dp", dp_count)
    return result / total_docs


def solution(mesh):
    placed = (P("dp", None), P("dp", None), P(("dp", "land"), None), P(), P(("dp", "land"), None))
    return jax.shard_map(
        on_device, mesh=mesh, in_specs=placed, out_specs=P(("dp", "land"), None), check_vma=False
    )
```

```python
import jax
import jax.numpy as jnp
from jax import lax
from jax.experimental import pallas as pl
from jax.experimental.pallas import tpu as pltpu
from jax.sharding import PartitionSpec as P

TERM_BLOCK = 128
ACTIVE = 8
LAND_ACTIVE = 8
DOC_BLOCK = 128
LM_BLOCK = 128


sharpness = 2.0


def split_pair(values):
    high = lax.optimization_barrier(values.astype(jnp.bfloat16))
    low = (values - high.astype(jnp.float32)).astype(jnp.bfloat16)
    return (high, low)


def match_table(doc_blocks, land_ids):
    eq = doc_blocks[None, :, :, None] == land_ids[:, None, None, :]
    has = jnp.any(eq, axis=2)
    first = jnp.argmax(eq, axis=2).astype(jnp.int32)
    return jnp.where(has, first, ACTIVE).astype(jnp.int32).reshape(-1)


def forward_kernel(slot_ref, doc_ref, dn_ref, land_ref,
                   high_ref, low_ref, fit_ref, aligned_ref):
    step = pl.program_id(0)
    doc_count = dn_ref.shape[0] // DOC_BLOCK

    @pl.when(step == 0)
    def _():
        fit_ref[...] = jnp.zeros_like(fit_ref)

    for d in range(doc_count):
        for b in range(LAND_ACTIVE):
            a = slot_ref[(step * doc_count + d) * LAND_ACTIVE + b]
            aligned_ref[d * DOC_BLOCK:(d + 1) * DOC_BLOCK, b * TERM_BLOCK:(b + 1) * TERM_BLOCK] = (
                doc_ref[d * (ACTIVE + 1) + a])
    width = ACTIVE * TERM_BLOCK
    tile = land_ref[:, :width]
    squares = jnp.zeros((LM_BLOCK, TERM_BLOCK), jnp.float32)
    for b in range(LAND_ACTIVE):
        part = tile[:, b * TERM_BLOCK:(b + 1) * TERM_BLOCK].astype(jnp.float32)
        squares = squares + part * part
    land_norm = lax.rsqrt(jnp.sum(squares.T, axis=0, keepdims=True) + 1e-06)
    inner = lax.dot_general(
        aligned_ref[...], tile, (((1,), (1,)), ((), ())),
        preferred_element_type=jnp.float32)
    cosine = inner * dn_ref[...] * land_norm
    kern = jnp.exp(2.0 * sharpness * (cosine - 1.0))
    high = kern.astype(jnp.bfloat16)
    low = (kern - high.astype(jnp.float32)).astype(jnp.bfloat16)
    high_ref[...] = high
    low_ref[...] = low
    coef = land_ref[:, width:]
    part = jnp.dot(high, coef, preferred_element_type=jnp.float32)
    part = part + jnp.dot(low, coef, preferred_element_type=jnp.float32)
    fit_ref[...] += part


def forward(slots, doc_tiles, doc_norm, land_rows, targets):
    doc_rows = doc_norm.shape[0]
    land_count = land_rows.shape[0]
    block_count = land_count // LM_BLOCK
    width = ACTIVE * TERM_BLOCK
    grid_spec = pltpu.PrefetchScalarGridSpec(
        num_scalar_prefetch=1,
        grid=(block_count,),
        in_specs=[
            pl.BlockSpec(doc_tiles.shape, lambda l, s: (0, 0, 0)),
            pl.BlockSpec((doc_rows, 1), lambda l, s: (0, 0)),
            pl.BlockSpec((LM_BLOCK, land_rows.shape[1]), lambda l, s: (l, 0)),
        ],
        out_specs=[
            pl.BlockSpec((doc_rows, LM_BLOCK), lambda l, s: (0, l)),
            pl.BlockSpec((doc_rows, LM_BLOCK), lambda l, s: (0, l)),
            pl.BlockSpec((doc_rows, targets), lambda l, s: (0, 0)),
        ],
        scratch_shapes=[pltpu.VMEM((doc_rows, width), jnp.bfloat16)],
    )
    return pl.pallas_call(
        forward_kernel,
        grid_spec=grid_spec,
        out_shape=[
            jax.ShapeDtypeStruct((doc_rows, land_count), jnp.bfloat16),
            jax.ShapeDtypeStruct((doc_rows, land_count), jnp.bfloat16),
            jax.ShapeDtypeStruct((doc_rows, targets), jnp.float32),
        ],
        compiler_params=pltpu.CompilerParams(
            dimension_semantics=("arbitrary",), vmem_limit_bytes=48 * 1024 * 1024),
    )(slots, doc_tiles, doc_norm, land_rows)


def gather_rows(rows, dp_count):
    own = lax.axis_index("dp")
    parts = [rows]
    sources = [own]
    for k in range(1, dp_count // 2):
        shift = [(i, (i + 2 * k) % dp_count) for i in range(dp_count)]
        parts.append(lax.ppermute(rows, "dp", shift))
        sources.append((own - 2 * k) % dp_count)
    mine = jnp.concatenate(parts, axis=0)
    other = lax.ppermute(mine, "dp", [(i, i ^ 1) for i in range(dp_count)])
    sources = sources + [s ^ 1 for s in sources]
    return jnp.concatenate([mine, other], axis=0), jnp.stack(sources).astype(jnp.int32)


def scatter_sum(pieces, axis, count):
    own = lax.axis_index(axis)
    total = lax.dynamic_index_in_dim(pieces, own, axis=0, keepdims=False)
    for k in range(1, count):
        shift = [(i, (i + k) % count) for i in range(count)]
        piece = lax.dynamic_index_in_dim(pieces, (own + k) % count, axis=0, keepdims=False)
        total = total + lax.ppermute(piece, axis, shift)
    return total


def gather_all(piece, axis, count):
    own = lax.axis_index(axis)
    got = [piece]
    for k in range(1, count):
        got.append(lax.ppermute(piece, axis, [(i, (i + k) % count) for i in range(count)]))
    got = jnp.stack(got)
    order = (own - jnp.arange(count)) % count
    return got[order]


def all_sum(values, axis, count):
    pieces = values.reshape((count, values.shape[0] // count) + values.shape[1:])
    mine = scatter_sum(pieces, axis, count)
    return gather_all(mine, axis, count).reshape(values.shape)


def on_device(doc_values, doc_blocks, land_values, land_blocks, coefficients):
    dp_count = lax.axis_size("dp")
    land_count = lax.axis_size("land")
    doc_rows = doc_values.shape[0]
    targets = coefficients.shape[1]
    total_docs = doc_rows * dp_count
    own_blocks = land_values.shape[0] // LM_BLOCK
    doc_count = doc_rows // DOC_BLOCK
    doc_norm = lax.rsqrt(jnp.sum(jnp.square(doc_values.astype(jnp.float32)), axis=1) + 1e-06)
    table = land_blocks.reshape(dp_count, land_count, own_blocks, LAND_ACTIVE)
    own_table = lax.dynamic_index_in_dim(table, lax.axis_index("land"), axis=1, keepdims=False)
    own_table = own_table.reshape(dp_count * own_blocks, LAND_ACTIVE)
    land_rows, sources = gather_rows(jnp.concatenate([land_values, coefficients], axis=1), dp_count)
    own_table = own_table[sources]
    doc_tiles = doc_values.reshape(doc_count, DOC_BLOCK, ACTIVE, TERM_BLOCK).transpose(0, 2, 1, 3)
    doc_tiles = jnp.pad(doc_tiles, ((0, 0), (0, 1), (0, 0), (0, 0)))
    doc_tiles = doc_tiles.reshape(doc_count * (ACTIVE + 1), DOC_BLOCK, TERM_BLOCK)
    slots = match_table(doc_blocks, own_table)
    tile_high, tile_low, fitted = forward(
        slots, doc_tiles, doc_norm.reshape(doc_rows, 1), land_rows, targets)
    fitted = all_sum(fitted, "land", land_count)
    fitted_high, fitted_low = split_pair(fitted)
    fitted_pair = jnp.concatenate([fitted_high, fitted_low], axis=1)
    summed = jnp.dot(tile_high.T, fitted_pair, preferred_element_type=jnp.float32)
    summed = summed + jnp.dot(tile_low.T, fitted_pair, preferred_element_type=jnp.float32)
    summed = summed[:, :targets] + summed[:, targets:]
    order = jnp.argsort(sources)
    summed = summed.reshape(dp_count, own_blocks * LM_BLOCK, targets)[order]
    result = scatter_sum(summed, "dp", dp_count)
    return result / total_docs


def solution(mesh):
    placed = (P("dp", None), P("dp", None), P(("dp", "land"), None), P(), P(("dp", "land"), None))
    return jax.shard_map(
        on_device, mesh=mesh, in_specs=placed, out_specs=P(("dp", "land"), None), check_vma=False
    )
```

```python
import jax
import jax.numpy as jnp
from jax import lax
from jax.experimental import pallas as pl
from jax.experimental.pallas import tpu as pltpu
from jax.sharding import PartitionSpec as P

TERM_BLOCK = 128
ACTIVE = 8
LAND_ACTIVE = 8
DOC_BLOCK = 128
LM_BLOCK = 128


sharpness = 2.0


def split_pair(values):
    high = lax.optimization_barrier(values.astype(jnp.bfloat16))
    low = (values - high.astype(jnp.float32)).astype(jnp.bfloat16)
    return (high, low)


def match_table(doc_blocks, land_ids):
    eq = doc_blocks[None, :, :, None] == land_ids[:, None, None, :]
    has = jnp.any(eq, axis=2)
    first = jnp.argmax(eq, axis=2).astype(jnp.int32)
    return jnp.where(has, first, ACTIVE).astype(jnp.int32).reshape(-1)


def forward_kernel(slot_ref, doc_ref, dn_ref, land_ref,
                   high_ref, low_ref, fit_ref, aligned_ref):
    step = pl.program_id(0)
    doc_count = dn_ref.shape[0] // DOC_BLOCK

    @pl.when(step == 0)
    def _():
        fit_ref[...] = jnp.zeros_like(fit_ref)

    for d in range(doc_count):
        for b in range(LAND_ACTIVE):
            a = slot_ref[(step * doc_count + d) * LAND_ACTIVE + b]
            aligned_ref[d * DOC_BLOCK:(d + 1) * DOC_BLOCK, b * TERM_BLOCK:(b + 1) * TERM_BLOCK] = (
                doc_ref[d * (ACTIVE + 1) + a])
    width = ACTIVE * TERM_BLOCK
    tile = land_ref[:, :width]
    squares = jnp.zeros((LM_BLOCK, TERM_BLOCK), jnp.float32)
    for b in range(LAND_ACTIVE):
        part = tile[:, b * TERM_BLOCK:(b + 1) * TERM_BLOCK].astype(jnp.float32)
        squares = squares + part * part
    land_norm = lax.rsqrt(jnp.sum(squares.T, axis=0, keepdims=True) + 1e-06)
    inner = lax.dot_general(
        aligned_ref[...], tile, (((1,), (1,)), ((), ())),
        preferred_element_type=jnp.float32)
    cosine = inner * dn_ref[...] * land_norm
    kern = jnp.exp(2.0 * sharpness * (cosine - 1.0))
    high = kern.astype(jnp.bfloat16)
    low = (kern - high.astype(jnp.float32)).astype(jnp.bfloat16)
    high_ref[...] = high
    low_ref[...] = low
    coef = land_ref[:, width:]
    part = jnp.dot(high, coef, preferred_element_type=jnp.float32)
    part = part + jnp.dot(low, coef, preferred_element_type=jnp.float32)
    fit_ref[...] += part


def forward(slots, doc_tiles, doc_norm, land_rows, targets):
    doc_rows = doc_norm.shape[0]
    land_count = land_rows.shape[0]
    block_count = land_count // LM_BLOCK
    width = ACTIVE * TERM_BLOCK
    grid_spec = pltpu.PrefetchScalarGridSpec(
        num_scalar_prefetch=1,
        grid=(block_count,),
        in_specs=[
            pl.BlockSpec(doc_tiles.shape, lambda l, s: (0, 0, 0)),
            pl.BlockSpec((doc_rows, 1), lambda l, s: (0, 0)),
            pl.BlockSpec((LM_BLOCK, land_rows.shape[1]), lambda l, s: (l, 0)),
        ],
        out_specs=[
            pl.BlockSpec((doc_rows, LM_BLOCK), lambda l, s: (0, l)),
            pl.BlockSpec((doc_rows, LM_BLOCK), lambda l, s: (0, l)),
            pl.BlockSpec((doc_rows, targets), lambda l, s: (0, 0)),
        ],
        scratch_shapes=[pltpu.VMEM((doc_rows, width), jnp.bfloat16)],
    )
    return pl.pallas_call(
        forward_kernel,
        grid_spec=grid_spec,
        out_shape=[
            jax.ShapeDtypeStruct((doc_rows, land_count), jnp.bfloat16),
            jax.ShapeDtypeStruct((doc_rows, land_count), jnp.bfloat16),
            jax.ShapeDtypeStruct((doc_rows, targets), jnp.float32),
        ],
        compiler_params=pltpu.CompilerParams(
            dimension_semantics=("arbitrary",), vmem_limit_bytes=48 * 1024 * 1024),
    )(slots, doc_tiles, doc_norm, land_rows)


def sum_over(values, axis, count):
    pieces = values.reshape((count, values.shape[0] // count) + values.shape[1:])
    pieces = lax.all_to_all(pieces, axis, 0, 0, tiled=False)
    return jnp.sum(pieces, axis=0)


def all_sum(values, axis, count):
    mine = sum_over(values, axis, count)
    spread = jnp.broadcast_to(mine[None], (count,) + mine.shape)
    return lax.all_to_all(spread, axis, 0, 0, tiled=False).reshape(values.shape)


def on_device(doc_values, doc_blocks, land_values, land_blocks, coefficients):
    dp_count = lax.axis_size("dp")
    land_count = lax.axis_size("land")
    doc_rows = doc_values.shape[0]
    targets = coefficients.shape[1]
    total_docs = doc_rows * dp_count
    own_blocks = land_values.shape[0] // LM_BLOCK
    doc_count = doc_rows // DOC_BLOCK
    doc_norm = lax.rsqrt(jnp.sum(jnp.square(doc_values.astype(jnp.float32)), axis=1) + 1e-06)
    table = land_blocks.reshape(dp_count, land_count, own_blocks, LAND_ACTIVE)
    own_table = lax.dynamic_index_in_dim(table, lax.axis_index("land"), axis=1, keepdims=False)
    own_table = own_table.reshape(dp_count * own_blocks, LAND_ACTIVE)
    land_rows = lax.all_gather(
        jnp.concatenate([land_values, coefficients], axis=1), "dp", axis=0, tiled=True)
    doc_tiles = doc_values.reshape(doc_count, DOC_BLOCK, ACTIVE, TERM_BLOCK).transpose(0, 2, 1, 3)
    doc_tiles = jnp.pad(doc_tiles, ((0, 0), (0, 1), (0, 0), (0, 0)))
    doc_tiles = doc_tiles.reshape(doc_count * (ACTIVE + 1), DOC_BLOCK, TERM_BLOCK)
    slots = match_table(doc_blocks, own_table)
    tile_high, tile_low, fitted = forward(
        slots, doc_tiles, doc_norm.reshape(doc_rows, 1), land_rows, targets)
    fitted = all_sum(fitted, "land", land_count)
    fitted_high, fitted_low = split_pair(fitted)
    fitted_pair = jnp.concatenate([fitted_high, fitted_low], axis=1)
    summed = jnp.dot(tile_high.T, fitted_pair, preferred_element_type=jnp.float32)
    summed = summed + jnp.dot(tile_low.T, fitted_pair, preferred_element_type=jnp.float32)
    summed = summed[:, :targets] + summed[:, targets:]
    result = sum_over(summed, "dp", dp_count)
    return result / total_docs


def solution(mesh):
    placed = (P("dp", None), P("dp", None), P(("dp", "land"), None), P(), P(("dp", "land"), None))
    return jax.shard_map(
        on_device, mesh=mesh, in_specs=placed, out_specs=P(("dp", "land"), None), check_vma=False
    )
```

```python
import jax
import jax.numpy as jnp
from jax import lax
from jax.experimental import pallas as pl
from jax.experimental.pallas import tpu as pltpu
from jax.sharding import PartitionSpec as P

TERM_BLOCK = 128
ACTIVE = 8
LAND_ACTIVE = 8
DOC_BLOCK = 128
LM_BLOCK = 128


sharpness = 2.0


def split_pair(values):
    high = lax.optimization_barrier(values.astype(jnp.bfloat16))
    low = (values - high.astype(jnp.float32)).astype(jnp.bfloat16)
    return (high, low)


def match_table(doc_blocks, land_ids):
    eq = doc_blocks[None, :, :, None] == land_ids[:, None, None, :]
    has = jnp.any(eq, axis=2)
    first = jnp.argmax(eq, axis=2).astype(jnp.int32)
    return jnp.where(has, first, ACTIVE).astype(jnp.int32).reshape(-1)


def forward_kernel(slot_ref, doc_ref, dn_ref, land_ref,
                   high_ref, low_ref, fit_ref, aligned_ref):
    step = pl.program_id(0)
    doc_count = dn_ref.shape[0] // DOC_BLOCK

    @pl.when(step == 0)
    def _():
        fit_ref[...] = jnp.zeros_like(fit_ref)

    for d in range(doc_count):
        for b in range(LAND_ACTIVE):
            a = slot_ref[(step * doc_count + d) * LAND_ACTIVE + b]
            aligned_ref[d * DOC_BLOCK:(d + 1) * DOC_BLOCK, b * TERM_BLOCK:(b + 1) * TERM_BLOCK] = (
                doc_ref[d * (ACTIVE + 1) + a])
    width = ACTIVE * TERM_BLOCK
    tile = land_ref[:, :width]
    squares = jnp.zeros((LM_BLOCK, TERM_BLOCK), jnp.float32)
    for b in range(LAND_ACTIVE):
        part = tile[:, b * TERM_BLOCK:(b + 1) * TERM_BLOCK].astype(jnp.float32)
        squares = squares + part * part
    land_norm = lax.rsqrt(jnp.sum(squares.T, axis=0, keepdims=True) + 1e-06)
    inner = lax.dot_general(
        aligned_ref[...], tile, (((1,), (1,)), ((), ())),
        preferred_element_type=jnp.float32)
    cosine = inner * dn_ref[...] * land_norm
    kern = jnp.exp(2.0 * sharpness * (cosine - 1.0))
    high = kern.astype(jnp.bfloat16)
    low = (kern - high.astype(jnp.float32)).astype(jnp.bfloat16)
    high_ref[...] = high
    low_ref[...] = low
    coef = land_ref[:, width:]
    part = jnp.dot(high, coef, preferred_element_type=jnp.float32)
    part = part + jnp.dot(low, coef, preferred_element_type=jnp.float32)
    fit_ref[...] += part


def forward(slots, doc_tiles, doc_norm, land_rows, targets):
    doc_rows = doc_norm.shape[0]
    land_count = land_rows.shape[0]
    block_count = land_count // LM_BLOCK
    width = ACTIVE * TERM_BLOCK
    grid_spec = pltpu.PrefetchScalarGridSpec(
        num_scalar_prefetch=1,
        grid=(block_count,),
        in_specs=[
            pl.BlockSpec(doc_tiles.shape, lambda l, s: (0, 0, 0)),
            pl.BlockSpec((doc_rows, 1), lambda l, s: (0, 0)),
            pl.BlockSpec((LM_BLOCK, land_rows.shape[1]), lambda l, s: (l, 0)),
        ],
        out_specs=[
            pl.BlockSpec((doc_rows, LM_BLOCK), lambda l, s: (0, l)),
            pl.BlockSpec((doc_rows, LM_BLOCK), lambda l, s: (0, l)),
            pl.BlockSpec((doc_rows, targets), lambda l, s: (0, 0)),
        ],
        scratch_shapes=[pltpu.VMEM((doc_rows, width), jnp.bfloat16)],
    )
    return pl.pallas_call(
        forward_kernel,
        grid_spec=grid_spec,
        out_shape=[
            jax.ShapeDtypeStruct((doc_rows, land_count), jnp.bfloat16),
            jax.ShapeDtypeStruct((doc_rows, land_count), jnp.bfloat16),
            jax.ShapeDtypeStruct((doc_rows, targets), jnp.float32),
        ],
        compiler_params=pltpu.CompilerParams(
            dimension_semantics=("arbitrary",), vmem_limit_bytes=48 * 1024 * 1024),
    )(slots, doc_tiles, doc_norm, land_rows)


def sum_over(values, axis, count):
    pieces = values.reshape((count, values.shape[0] // count) + values.shape[1:])
    pieces = lax.all_to_all(pieces, axis, 0, 0, tiled=False)
    return jnp.sum(pieces, axis=0)


def all_sum(values, axis, count):
    mine = sum_over(values, axis, count)
    spread = jnp.broadcast_to(mine[None], (count,) + mine.shape)
    return lax.all_to_all(spread, axis, 0, 0, tiled=False).reshape(values.shape)


def on_device(doc_values, doc_blocks, land_values, land_blocks, coefficients):
    dp_count = lax.axis_size("dp")
    land_count = lax.axis_size("land")
    doc_rows = doc_values.shape[0]
    targets = coefficients.shape[1]
    total_docs = doc_rows * dp_count
    own_blocks = land_values.shape[0] // LM_BLOCK
    doc_count = doc_rows // DOC_BLOCK
    doc_norm = lax.rsqrt(jnp.sum(jnp.square(doc_values.astype(jnp.float32)), axis=1) + 1e-06)
    table = land_blocks.reshape(dp_count, land_count, own_blocks, LAND_ACTIVE)
    own_table = lax.dynamic_index_in_dim(table, lax.axis_index("land"), axis=1, keepdims=False)
    own_table = own_table.reshape(dp_count * own_blocks, LAND_ACTIVE)
    rows = jnp.concatenate([land_values, coefficients], axis=1)
    core = lax.axis_index("dp") % 2
    groups = [list(range(c, dp_count, 2)) for c in range(2)]
    mine = lax.all_gather(rows, "dp", axis=0, tiled=True, axis_index_groups=groups)
    other = lax.ppermute(mine, "dp", [(i, i ^ 1) for i in range(dp_count)])
    half = dp_count // 2
    sources = jnp.concatenate([core + 2 * jnp.arange(half), (1 - core) + 2 * jnp.arange(half)])
    own_table = own_table.reshape(dp_count, own_blocks, LAND_ACTIVE)[sources]
    own_table = own_table.reshape(-1, LAND_ACTIVE)
    split = half * own_blocks
    doc_tiles = doc_values.reshape(doc_count, DOC_BLOCK, ACTIVE, TERM_BLOCK).transpose(0, 2, 1, 3)
    doc_tiles = jnp.pad(doc_tiles, ((0, 0), (0, 1), (0, 0), (0, 0)))
    doc_tiles = doc_tiles.reshape(doc_count * (ACTIVE + 1), DOC_BLOCK, TERM_BLOCK)
    doc_norm = doc_norm.reshape(doc_rows, 1)
    high_one, low_one, fitted_one = forward(
        match_table(doc_blocks, own_table[:split]), doc_tiles, doc_norm, mine, targets)
    high_two, low_two, fitted_two = forward(
        match_table(doc_blocks, own_table[split:]), doc_tiles, doc_norm, other, targets)
    fitted = all_sum(fitted_one + fitted_two, "land", land_count)
    fitted_high, fitted_low = split_pair(fitted)
    fitted_pair = jnp.concatenate([fitted_high, fitted_low], axis=1)
    summed = []
    for tile_high, tile_low in ((high_one, low_one), (high_two, low_two)):
        part = jnp.dot(tile_high.T, fitted_pair, preferred_element_type=jnp.float32)
        part = part + jnp.dot(tile_low.T, fitted_pair, preferred_element_type=jnp.float32)
        summed.append(part[:, :targets] + part[:, targets:])
    summed = jnp.concatenate(summed, axis=0).reshape(dp_count, -1, targets)
    summed = summed[jnp.argsort(sources)]
    result = sum_over(summed.reshape(-1, targets), "dp", dp_count)
    return result / total_docs


def solution(mesh):
    placed = (P("dp", None), P("dp", None), P(("dp", "land"), None), P(), P(("dp", "land"), None))
    return jax.shard_map(
        on_device, mesh=mesh, in_specs=placed, out_specs=P(("dp", "land"), None), check_vma=False
    )
```

```python
import jax
import jax.numpy as jnp
from jax import lax
from jax.experimental import pallas as pl
from jax.experimental.pallas import tpu as pltpu
from jax.sharding import PartitionSpec as P

TERM_BLOCK = 128
ACTIVE = 8
LAND_ACTIVE = 8
DOC_BLOCK = 128
LM_BLOCK = 128


sharpness = 2.0


def split_pair(values):
    high = lax.optimization_barrier(values.astype(jnp.bfloat16))
    low = (values - high.astype(jnp.float32)).astype(jnp.bfloat16)
    return (high, low)


def match_table(doc_blocks, land_ids):
    eq = doc_blocks[None, :, :, None] == land_ids[:, None, None, :]
    has = jnp.any(eq, axis=2)
    first = jnp.argmax(eq, axis=2).astype(jnp.int32)
    return jnp.where(has, first, ACTIVE).astype(jnp.int32).reshape(-1)


def forward_kernel(slot_ref, doc_ref, dn_ref, land_ref,
                   high_ref, low_ref, fit_ref, aligned_ref):
    step = pl.program_id(0)
    doc_count = dn_ref.shape[0] // DOC_BLOCK

    @pl.when(step == 0)
    def _():
        fit_ref[...] = jnp.zeros_like(fit_ref)

    for d in range(doc_count):
        for b in range(LAND_ACTIVE):
            a = slot_ref[(step * doc_count + d) * LAND_ACTIVE + b]
            aligned_ref[d * DOC_BLOCK:(d + 1) * DOC_BLOCK, b * TERM_BLOCK:(b + 1) * TERM_BLOCK] = (
                doc_ref[d * (ACTIVE + 1) + a])
    width = ACTIVE * TERM_BLOCK
    tile = land_ref[:, :width]
    squares = jnp.zeros((LM_BLOCK, TERM_BLOCK), jnp.float32)
    for b in range(LAND_ACTIVE):
        part = tile[:, b * TERM_BLOCK:(b + 1) * TERM_BLOCK].astype(jnp.float32)
        squares = squares + part * part
    land_norm = lax.rsqrt(jnp.sum(squares.T, axis=0, keepdims=True) + 1e-06)
    inner = lax.dot_general(
        aligned_ref[...], tile, (((1,), (1,)), ((), ())),
        preferred_element_type=jnp.float32)
    cosine = inner * dn_ref[...] * land_norm
    kern = jnp.exp(2.0 * sharpness * (cosine - 1.0))
    high = kern.astype(jnp.bfloat16)
    low = (kern - high.astype(jnp.float32)).astype(jnp.bfloat16)
    high_ref[...] = high
    low_ref[...] = low
    coef = land_ref[:, width:]
    part = jnp.dot(high, coef, preferred_element_type=jnp.float32)
    part = part + jnp.dot(low, coef, preferred_element_type=jnp.float32)
    fit_ref[...] += part


def forward(slots, doc_tiles, doc_norm, land_rows, targets):
    doc_rows = doc_norm.shape[0]
    land_count = land_rows.shape[0]
    block_count = land_count // LM_BLOCK
    width = ACTIVE * TERM_BLOCK
    grid_spec = pltpu.PrefetchScalarGridSpec(
        num_scalar_prefetch=1,
        grid=(block_count,),
        in_specs=[
            pl.BlockSpec(doc_tiles.shape, lambda l, s: (0, 0, 0)),
            pl.BlockSpec((doc_rows, 1), lambda l, s: (0, 0)),
            pl.BlockSpec((LM_BLOCK, land_rows.shape[1]), lambda l, s: (l, 0)),
        ],
        out_specs=[
            pl.BlockSpec((doc_rows, LM_BLOCK), lambda l, s: (0, l)),
            pl.BlockSpec((doc_rows, LM_BLOCK), lambda l, s: (0, l)),
            pl.BlockSpec((doc_rows, targets), lambda l, s: (0, 0)),
        ],
        scratch_shapes=[pltpu.VMEM((doc_rows, width), jnp.bfloat16)],
    )
    return pl.pallas_call(
        forward_kernel,
        grid_spec=grid_spec,
        out_shape=[
            jax.ShapeDtypeStruct((doc_rows, land_count), jnp.bfloat16),
            jax.ShapeDtypeStruct((doc_rows, land_count), jnp.bfloat16),
            jax.ShapeDtypeStruct((doc_rows, targets), jnp.float32),
        ],
        compiler_params=pltpu.CompilerParams(
            dimension_semantics=("arbitrary",), vmem_limit_bytes=48 * 1024 * 1024),
    )(slots, doc_tiles, doc_norm, land_rows)


def sum_over(values, axis, count):
    pieces = values.reshape((count, values.shape[0] // count) + values.shape[1:])
    pieces = lax.all_to_all(pieces, axis, 0, 0, tiled=False)
    return jnp.sum(pieces, axis=0)


def all_sum(values, axis, count):
    mine = sum_over(values, axis, count)
    spread = jnp.broadcast_to(mine[None], (count,) + mine.shape)
    return lax.all_to_all(spread, axis, 0, 0, tiled=False).reshape(values.shape)


def on_device(doc_values, doc_blocks, land_values, land_blocks, coefficients):
    dp_count = lax.axis_size("dp")
    land_count = lax.axis_size("land")
    doc_rows = doc_values.shape[0]
    targets = coefficients.shape[1]
    total_docs = doc_rows * dp_count
    own_blocks = land_values.shape[0] // LM_BLOCK
    doc_count = doc_rows // DOC_BLOCK
    doc_norm = lax.rsqrt(jnp.sum(jnp.square(doc_values.astype(jnp.float32)), axis=1) + 1e-06)
    table = land_blocks.reshape(dp_count, land_count, own_blocks, LAND_ACTIVE)
    own_table = lax.dynamic_index_in_dim(table, lax.axis_index("land"), axis=1, keepdims=False)
    own_table = own_table.reshape(dp_count * own_blocks, LAND_ACTIVE)
    land_rows = lax.all_gather(
        jnp.concatenate([land_values, coefficients], axis=1), "dp", axis=0, tiled=True)
    doc_tiles = doc_values.reshape(doc_count, DOC_BLOCK, ACTIVE, TERM_BLOCK).transpose(0, 2, 1, 3)
    doc_tiles = jnp.pad(doc_tiles, ((0, 0), (0, 1), (0, 0), (0, 0)))
    doc_tiles = doc_tiles.reshape(doc_count * (ACTIVE + 1), DOC_BLOCK, TERM_BLOCK)
    doc_norm = doc_norm.reshape(doc_rows, 1)
    halves = 2
    step = doc_count // halves
    summed = None
    for h in range(halves):
        lo, hi = h * step, (h + 1) * step
        tile_high, tile_low, fitted = forward(
            match_table(doc_blocks[lo:hi], own_table), doc_tiles[lo * (ACTIVE + 1):hi * (ACTIVE + 1)],
            doc_norm[lo * DOC_BLOCK:hi * DOC_BLOCK], land_rows, targets)
        fitted = all_sum(fitted, "land", land_count)
        fitted_high, fitted_low = split_pair(fitted)
        fitted_pair = jnp.concatenate([fitted_high, fitted_low], axis=1)
        part = jnp.dot(tile_high.T, fitted_pair, preferred_element_type=jnp.float32)
        part = part + jnp.dot(tile_low.T, fitted_pair, preferred_element_type=jnp.float32)
        summed = part if summed is None else summed + part
    summed = summed[:, :targets] + summed[:, targets:]
    result = sum_over(summed, "dp", dp_count)
    return result / total_docs


def solution(mesh):
    placed = (P("dp", None), P("dp", None), P(("dp", "land"), None), P(), P(("dp", "land"), None))
    return jax.shard_map(
        on_device, mesh=mesh, in_specs=placed, out_specs=P(("dp", "land"), None), check_vma=False
    )
```

```python
import jax
import jax.numpy as jnp
from jax import lax
from jax.experimental import pallas as pl
from jax.experimental.pallas import tpu as pltpu
from jax.sharding import PartitionSpec as P

TERM_BLOCK = 128
ACTIVE = 8
LAND_ACTIVE = 8
DOC_BLOCK = 128
LM_BLOCK = 128


sharpness = 2.0


def split_pair(values):
    high = lax.optimization_barrier(values.astype(jnp.bfloat16))
    low = (values - high.astype(jnp.float32)).astype(jnp.bfloat16)
    return (high, low)


def match_table(doc_blocks, land_ids):
    eq = doc_blocks[None, :, :, None] == land_ids[:, None, None, :]
    has = jnp.any(eq, axis=2)
    first = jnp.argmax(eq, axis=2).astype(jnp.int32)
    return jnp.where(has, first, ACTIVE).astype(jnp.int32).reshape(-1)


def forward_kernel(slot_ref, doc_ref, dn_ref, land_ref,
                   high_ref, low_ref, fit_ref, aligned_ref):
    step = pl.program_id(0)
    doc_count = dn_ref.shape[0] // DOC_BLOCK

    @pl.when(step == 0)
    def _():
        fit_ref[...] = jnp.zeros_like(fit_ref)

    for d in range(doc_count):
        for b in range(LAND_ACTIVE):
            a = slot_ref[(step * doc_count + d) * LAND_ACTIVE + b]
            aligned_ref[d * DOC_BLOCK:(d + 1) * DOC_BLOCK, b * TERM_BLOCK:(b + 1) * TERM_BLOCK] = (
                doc_ref[d * (ACTIVE + 1) + a])
    width = ACTIVE * TERM_BLOCK
    tile = land_ref[:width, :]
    squares = tile.astype(jnp.float32)
    land_norm = lax.rsqrt(jnp.sum(squares * squares, axis=0, keepdims=True) + 1e-06)
    inner = jnp.dot(aligned_ref[...], tile, preferred_element_type=jnp.float32)
    kern = jnp.exp(inner * dn_ref[...] * land_norm - 2.0 * sharpness)
    high = kern.astype(jnp.bfloat16)
    low = (kern - high.astype(jnp.float32)).astype(jnp.bfloat16)
    high_ref[0] = high
    low_ref[0] = low
    coef = land_ref[width:, :]
    dims = (((1,), (1,)), ((), ()))
    part = lax.dot_general(high, coef, dims, preferred_element_type=jnp.float32)
    part = part + lax.dot_general(low, coef, dims, preferred_element_type=jnp.float32)
    fit_ref[...] += part


def forward(slots, doc_tiles, doc_norm, land_rows, targets):
    doc_rows = doc_norm.shape[0]
    row_height = ACTIVE * TERM_BLOCK + targets
    block_count = land_rows.shape[0] // row_height
    land_count = block_count * LM_BLOCK
    width = ACTIVE * TERM_BLOCK
    grid_spec = pltpu.PrefetchScalarGridSpec(
        num_scalar_prefetch=1,
        grid=(block_count,),
        in_specs=[
            pl.BlockSpec(doc_tiles.shape, lambda l, s: (0, 0, 0)),
            pl.BlockSpec((doc_rows, 1), lambda l, s: (0, 0)),
            pl.BlockSpec((row_height, LM_BLOCK), lambda l, s: (l, 0)),
        ],
        out_specs=[
            pl.BlockSpec((1, doc_rows, LM_BLOCK), lambda l, s: (l, 0, 0)),
            pl.BlockSpec((1, doc_rows, LM_BLOCK), lambda l, s: (l, 0, 0)),
            pl.BlockSpec((doc_rows, targets), lambda l, s: (0, 0)),
        ],
        scratch_shapes=[pltpu.VMEM((doc_rows, width), jnp.bfloat16)],
    )
    return pl.pallas_call(
        forward_kernel,
        grid_spec=grid_spec,
        out_shape=[
            jax.ShapeDtypeStruct((block_count, doc_rows, LM_BLOCK), jnp.bfloat16),
            jax.ShapeDtypeStruct((block_count, doc_rows, LM_BLOCK), jnp.bfloat16),
            jax.ShapeDtypeStruct((doc_rows, targets), jnp.float32),
        ],
        compiler_params=pltpu.CompilerParams(
            dimension_semantics=("arbitrary",), vmem_limit_bytes=48 * 1024 * 1024),
    )(slots, doc_tiles, doc_norm, land_rows)


def sum_over(values, axis, count):
    pieces = values.reshape((count, values.shape[0] // count) + values.shape[1:])
    pieces = lax.all_to_all(pieces, axis, 0, 0, tiled=False)
    return jnp.sum(pieces, axis=0)


def all_sum(values, axis, count):
    mine = sum_over(values, axis, count)
    spread = jnp.broadcast_to(mine[None], (count,) + mine.shape)
    return lax.all_to_all(spread, axis, 0, 0, tiled=False).reshape(values.shape)


def on_device(doc_values, doc_blocks, land_values, land_blocks, coefficients):
    dp_count = lax.axis_size("dp")
    land_count = lax.axis_size("land")
    doc_rows = doc_values.shape[0]
    targets = coefficients.shape[1]
    total_docs = doc_rows * dp_count
    own_blocks = land_values.shape[0] // LM_BLOCK
    doc_count = doc_rows // DOC_BLOCK
    doc_norm = lax.rsqrt(jnp.sum(jnp.square(doc_values.astype(jnp.float32)), axis=1) + 1e-06)
    table = land_blocks.reshape(dp_count, land_count, own_blocks, LAND_ACTIVE)
    own_table = lax.dynamic_index_in_dim(table, lax.axis_index("land"), axis=1, keepdims=False)
    own_table = own_table.reshape(dp_count * own_blocks, LAND_ACTIVE)
    land_rows = lax.all_gather(
        jnp.concatenate([land_values, coefficients], axis=1).T, "dp", axis=0, tiled=True)
    doc_tiles = doc_values.reshape(doc_count, DOC_BLOCK, ACTIVE, TERM_BLOCK).transpose(0, 2, 1, 3)
    doc_tiles = jnp.pad(doc_tiles, ((0, 0), (0, 1), (0, 0), (0, 0)))
    doc_tiles = doc_tiles.reshape(doc_count * (ACTIVE + 1), DOC_BLOCK, TERM_BLOCK)
    slots = match_table(doc_blocks, own_table)
    tile_high, tile_low, fitted = forward(
        slots, doc_tiles, (2.0 * sharpness) * doc_norm.reshape(doc_rows, 1), land_rows, targets)
    fitted = all_sum(fitted, "land", land_count)
    fitted_high, fitted_low = split_pair(fitted)
    fitted_pair = jnp.concatenate([fitted_high, fitted_low], axis=1)
    summed = jnp.einsum("qnl,nt->qlt", tile_high, fitted_pair, preferred_element_type=jnp.float32)
    summed = summed + jnp.einsum("qnl,nt->qlt", tile_low, fitted_pair, preferred_element_type=jnp.float32)
    summed = (summed[:, :, :targets] + summed[:, :, targets:]).reshape(-1, targets)
    result = sum_over(summed, "dp", dp_count)
    return result / total_docs


def solution(mesh):
    placed = (P("dp", None), P("dp", None), P(("dp", "land"), None), P(), P(("dp", "land"), None))
    return jax.shard_map(
        on_device, mesh=mesh, in_specs=placed, out_specs=P(("dp", "land"), None), check_vma=False
    )
```

```python
import jax
import jax.numpy as jnp
from jax import lax
from jax.experimental import pallas as pl
from jax.experimental.pallas import tpu as pltpu
from jax.sharding import PartitionSpec as P

TERM_BLOCK = 128
ACTIVE = 8
LAND_ACTIVE = 8
DOC_BLOCK = 128
LM_BLOCK = 128


sharpness = 2.0


def split_pair(values):
    high = lax.optimization_barrier(values.astype(jnp.bfloat16))
    low = (values - high.astype(jnp.float32)).astype(jnp.bfloat16)
    return (high, low)


def match_table(doc_blocks, land_ids):
    eq = doc_blocks[None, :, :, None] == land_ids[:, None, None, :]
    has = jnp.any(eq, axis=2)
    first = jnp.argmax(eq, axis=2).astype(jnp.int32)
    return jnp.where(has, first, ACTIVE).astype(jnp.int32).reshape(-1)


def forward_kernel(slot_ref, doc_ref, dn_ref, land_ref,
                   high_ref, low_ref, fit_ref, aligned_ref):
    step = pl.program_id(0)
    doc_count = dn_ref.shape[0] // DOC_BLOCK

    @pl.when(step == 0)
    def _():
        fit_ref[...] = jnp.zeros_like(fit_ref)

    for d in range(doc_count):
        for b in range(LAND_ACTIVE):
            a = slot_ref[(step * doc_count + d) * LAND_ACTIVE + b]
            aligned_ref[d * DOC_BLOCK:(d + 1) * DOC_BLOCK, b * TERM_BLOCK:(b + 1) * TERM_BLOCK] = (
                doc_ref[d * (ACTIVE + 1) + a])
    width = ACTIVE * TERM_BLOCK
    tile = land_ref[:width, :]
    squares = tile.astype(jnp.float32)
    land_norm = lax.rsqrt(jnp.sum(squares * squares, axis=0, keepdims=True) + 1e-06)
    inner = jnp.dot(aligned_ref[...], tile, preferred_element_type=jnp.float32)
    kern = jnp.exp(inner * dn_ref[...] * land_norm - 2.0 * sharpness)
    high = kern.astype(jnp.bfloat16)
    low = (kern - high.astype(jnp.float32)).astype(jnp.bfloat16)
    high_ref[0] = high
    low_ref[0] = low
    coef = land_ref[width:, :]
    dims = (((1,), (1,)), ((), ()))
    part = lax.dot_general(high, coef, dims, preferred_element_type=jnp.float32)
    part = part + lax.dot_general(low, coef, dims, preferred_element_type=jnp.float32)
    fit_ref[...] += part


def forward(slots, doc_tiles, doc_norm, land_rows, targets):
    doc_rows = doc_norm.shape[0]
    row_height = ACTIVE * TERM_BLOCK + targets
    block_count = land_rows.shape[0] // row_height
    land_count = block_count * LM_BLOCK
    width = ACTIVE * TERM_BLOCK
    grid_spec = pltpu.PrefetchScalarGridSpec(
        num_scalar_prefetch=1,
        grid=(block_count,),
        in_specs=[
            pl.BlockSpec(doc_tiles.shape, lambda l, s: (0, 0, 0)),
            pl.BlockSpec((doc_rows, 1), lambda l, s: (0, 0)),
            pl.BlockSpec((row_height, LM_BLOCK), lambda l, s: (l, 0)),
        ],
        out_specs=[
            pl.BlockSpec((1, doc_rows, LM_BLOCK), lambda l, s: (l, 0, 0)),
            pl.BlockSpec((1, doc_rows, LM_BLOCK), lambda l, s: (l, 0, 0)),
            pl.BlockSpec((doc_rows, targets), lambda l, s: (0, 0)),
        ],
        scratch_shapes=[pltpu.VMEM((doc_rows, width), jnp.bfloat16)],
    )
    return pl.pallas_call(
        forward_kernel,
        grid_spec=grid_spec,
        out_shape=[
            jax.ShapeDtypeStruct((block_count, doc_rows, LM_BLOCK), jnp.bfloat16),
            jax.ShapeDtypeStruct((block_count, doc_rows, LM_BLOCK), jnp.bfloat16),
            jax.ShapeDtypeStruct((doc_rows, targets), jnp.float32),
        ],
        compiler_params=pltpu.CompilerParams(
            dimension_semantics=("arbitrary",), vmem_limit_bytes=48 * 1024 * 1024),
    )(slots, doc_tiles, doc_norm, land_rows)


def sum_over(values, axis, count):
    pieces = values.reshape((count, values.shape[0] // count) + values.shape[1:])
    pieces = lax.all_to_all(pieces, axis, 0, 0, tiled=False)
    return jnp.sum(pieces, axis=0)


def all_sum(values, axis, count):
    mine = sum_over(values, axis, count)
    spread = jnp.broadcast_to(mine[None], (count,) + mine.shape)
    return lax.all_to_all(spread, axis, 0, 0, tiled=False).reshape(values.shape)


def on_device(doc_values, doc_blocks, land_values, land_blocks, coefficients):
    dp_count = lax.axis_size("dp")
    land_count = lax.axis_size("land")
    doc_rows = doc_values.shape[0]
    targets = coefficients.shape[1]
    total_docs = doc_rows * dp_count
    own_blocks = land_values.shape[0] // LM_BLOCK
    doc_count = doc_rows // DOC_BLOCK
    doc_norm = lax.rsqrt(jnp.sum(jnp.square(doc_values.astype(jnp.float32)), axis=1) + 1e-06)
    table = land_blocks.reshape(dp_count, land_count, own_blocks, LAND_ACTIVE)
    own_table = lax.dynamic_index_in_dim(table, lax.axis_index("land"), axis=1, keepdims=False)
    own_table = own_table.reshape(dp_count * own_blocks, LAND_ACTIVE)
    rows = jnp.concatenate([land_values, coefficients], axis=1).T
    land_rows = lax.all_to_all(
        jnp.broadcast_to(rows[None], (dp_count,) + rows.shape), "dp", 0, 0, tiled=False)
    land_rows = land_rows.reshape(-1, rows.shape[1])
    doc_tiles = doc_values.reshape(doc_count, DOC_BLOCK, ACTIVE, TERM_BLOCK).transpose(0, 2, 1, 3)
    doc_tiles = jnp.pad(doc_tiles, ((0, 0), (0, 1), (0, 0), (0, 0)))
    doc_tiles = doc_tiles.reshape(doc_count * (ACTIVE + 1), DOC_BLOCK, TERM_BLOCK)
    slots = match_table(doc_blocks, own_table)
    tile_high, tile_low, fitted = forward(
        slots, doc_tiles, (2.0 * sharpness) * doc_norm.reshape(doc_rows, 1), land_rows, targets)
    fitted = all_sum(fitted, "land", land_count)
    fitted_high, fitted_low = split_pair(fitted)
    fitted_pair = jnp.concatenate([fitted_high, fitted_low], axis=1)
    summed = jnp.einsum("qnl,nt->qlt", tile_high, fitted_pair, preferred_element_type=jnp.float32)
    summed = summed + jnp.einsum("qnl,nt->qlt", tile_low, fitted_pair, preferred_element_type=jnp.float32)
    summed = (summed[:, :, :targets] + summed[:, :, targets:]).reshape(-1, targets)
    result = sum_over(summed, "dp", dp_count)
    return result / total_docs


def solution(mesh):
    placed = (P("dp", None), P("dp", None), P(("dp", "land"), None), P(), P(("dp", "land"), None))
    return jax.shard_map(
        on_device, mesh=mesh, in_specs=placed, out_specs=P(("dp", "land"), None), check_vma=False
    )
```

```python
import jax
import jax.numpy as jnp
from jax import lax
from jax.experimental import pallas as pl
from jax.experimental.pallas import tpu as pltpu
from jax.sharding import PartitionSpec as P

TERM_BLOCK = 128
ACTIVE = 8
LAND_ACTIVE = 8
DOC_BLOCK = 128
LM_BLOCK = 128


sharpness = 2.0


def split_pair(values):
    high = lax.optimization_barrier(values.astype(jnp.bfloat16))
    low = (values - high.astype(jnp.float32)).astype(jnp.bfloat16)
    return (high, low)


def match_table(doc_blocks, land_ids):
    eq = doc_blocks[None, :, :, None] == land_ids[:, None, None, :]
    has = jnp.any(eq, axis=2)
    first = jnp.argmax(eq, axis=2).astype(jnp.int32)
    return jnp.where(has, first, ACTIVE).astype(jnp.int32).reshape(-1)


GROUP = 2


def forward_kernel(slot_ref, doc_ref, dn_ref, land_ref,
                   high_ref, low_ref, fit_ref, aligned_ref):
    step = pl.program_id(0)
    doc_count = dn_ref.shape[0] // DOC_BLOCK
    width = ACTIVE * TERM_BLOCK
    row_height = land_ref.shape[0] // GROUP

    @pl.when(step == 0)
    def _():
        fit_ref[...] = jnp.zeros_like(fit_ref)

    for g in range(GROUP):
        block = step * GROUP + g
        for d in range(doc_count):
            for b in range(LAND_ACTIVE):
                a = slot_ref[(block * doc_count + d) * LAND_ACTIVE + b]
                aligned_ref[g, d * DOC_BLOCK:(d + 1) * DOC_BLOCK, b * TERM_BLOCK:(b + 1) * TERM_BLOCK] = (
                    doc_ref[d * (ACTIVE + 1) + a])
    for g in range(GROUP):
        top = g * row_height
        tile = land_ref[top:top + width, :]
        squares = tile.astype(jnp.float32)
        land_norm = lax.rsqrt(jnp.sum(squares * squares, axis=0, keepdims=True) + 1e-06)
        inner = jnp.dot(aligned_ref[g], tile, preferred_element_type=jnp.float32)
        kern = jnp.exp(inner * dn_ref[...] * land_norm - 2.0 * sharpness)
        high = kern.astype(jnp.bfloat16)
        low = (kern - high.astype(jnp.float32)).astype(jnp.bfloat16)
        high_ref[g] = high
        low_ref[g] = low
        coef = land_ref[top + width:top + row_height, :]
        dims = (((1,), (1,)), ((), ()))
        part = lax.dot_general(high, coef, dims, preferred_element_type=jnp.float32)
        part = part + lax.dot_general(low, coef, dims, preferred_element_type=jnp.float32)
        fit_ref[...] += part


def forward(slots, doc_tiles, doc_norm, land_rows, targets):
    doc_rows = doc_norm.shape[0]
    row_height = ACTIVE * TERM_BLOCK + targets
    block_count = land_rows.shape[0] // row_height
    land_count = block_count * LM_BLOCK
    width = ACTIVE * TERM_BLOCK
    grid_spec = pltpu.PrefetchScalarGridSpec(
        num_scalar_prefetch=1,
        grid=(block_count // GROUP,),
        in_specs=[
            pl.BlockSpec(doc_tiles.shape, lambda l, s: (0, 0, 0)),
            pl.BlockSpec((doc_rows, 1), lambda l, s: (0, 0)),
            pl.BlockSpec((GROUP * row_height, LM_BLOCK), lambda l, s: (l, 0)),
        ],
        out_specs=[
            pl.BlockSpec((GROUP, doc_rows, LM_BLOCK), lambda l, s: (l, 0, 0)),
            pl.BlockSpec((GROUP, doc_rows, LM_BLOCK), lambda l, s: (l, 0, 0)),
            pl.BlockSpec((doc_rows, targets), lambda l, s: (0, 0)),
        ],
        scratch_shapes=[pltpu.VMEM((GROUP, doc_rows, width), jnp.bfloat16)],
    )
    return pl.pallas_call(
        forward_kernel,
        grid_spec=grid_spec,
        out_shape=[
            jax.ShapeDtypeStruct((block_count, doc_rows, LM_BLOCK), jnp.bfloat16),
            jax.ShapeDtypeStruct((block_count, doc_rows, LM_BLOCK), jnp.bfloat16),
            jax.ShapeDtypeStruct((doc_rows, targets), jnp.float32),
        ],
        compiler_params=pltpu.CompilerParams(
            dimension_semantics=("arbitrary",), vmem_limit_bytes=48 * 1024 * 1024),
    )(slots, doc_tiles, doc_norm, land_rows)


def sum_over(values, axis, count):
    pieces = values.reshape((count, values.shape[0] // count) + values.shape[1:])
    pieces = lax.all_to_all(pieces, axis, 0, 0, tiled=False)
    return jnp.sum(pieces, axis=0)


def all_sum(values, axis, count):
    mine = sum_over(values, axis, count)
    spread = jnp.broadcast_to(mine[None], (count,) + mine.shape)
    return lax.all_to_all(spread, axis, 0, 0, tiled=False).reshape(values.shape)


def on_device(doc_values, doc_blocks, land_values, land_blocks, coefficients):
    dp_count = lax.axis_size("dp")
    land_count = lax.axis_size("land")
    doc_rows = doc_values.shape[0]
    targets = coefficients.shape[1]
    total_docs = doc_rows * dp_count
    own_blocks = land_values.shape[0] // LM_BLOCK
    doc_count = doc_rows // DOC_BLOCK
    doc_norm = lax.rsqrt(jnp.sum(jnp.square(doc_values.astype(jnp.float32)), axis=1) + 1e-06)
    table = land_blocks.reshape(dp_count, land_count, own_blocks, LAND_ACTIVE)
    own_table = lax.dynamic_index_in_dim(table, lax.axis_index("land"), axis=1, keepdims=False)
    own_table = own_table.reshape(dp_count * own_blocks, LAND_ACTIVE)
    land_rows = lax.all_gather(
        jnp.concatenate([land_values, coefficients], axis=1).T, "dp", axis=0, tiled=True)
    doc_tiles = doc_values.reshape(doc_count, DOC_BLOCK, ACTIVE, TERM_BLOCK).transpose(0, 2, 1, 3)
    doc_tiles = jnp.pad(doc_tiles, ((0, 0), (0, 1), (0, 0), (0, 0)))
    doc_tiles = doc_tiles.reshape(doc_count * (ACTIVE + 1), DOC_BLOCK, TERM_BLOCK)
    slots = match_table(doc_blocks, own_table)
    tile_high, tile_low, fitted = forward(
        slots, doc_tiles, (2.0 * sharpness) * doc_norm.reshape(doc_rows, 1), land_rows, targets)
    fitted = all_sum(fitted, "land", land_count)
    fitted_high, fitted_low = split_pair(fitted)
    fitted_pair = jnp.concatenate([fitted_high, fitted_low], axis=1)
    summed = jnp.einsum("qnl,nt->qlt", tile_high, fitted_pair, preferred_element_type=jnp.float32)
    summed = summed + jnp.einsum("qnl,nt->qlt", tile_low, fitted_pair, preferred_element_type=jnp.float32)
    summed = (summed[:, :, :targets] + summed[:, :, targets:]).reshape(-1, targets)
    result = sum_over(summed, "dp", dp_count)
    return result / total_docs


def solution(mesh):
    placed = (P("dp", None), P("dp", None), P(("dp", "land"), None), P(), P(("dp", "land"), None))
    return jax.shard_map(
        on_device, mesh=mesh, in_specs=placed, out_specs=P(("dp", "land"), None), check_vma=False
    )
```

```python
import jax
import jax.numpy as jnp
from jax import lax
from jax.experimental import pallas as pl
from jax.experimental.pallas import tpu as pltpu
from jax.sharding import PartitionSpec as P

TERM_BLOCK = 128
ACTIVE = 8
LAND_ACTIVE = 8
DOC_BLOCK = 128
LM_BLOCK = 128


sharpness = 2.0


def split_pair(values):
    high = lax.optimization_barrier(values.astype(jnp.bfloat16))
    low = (values - high.astype(jnp.float32)).astype(jnp.bfloat16)
    return (high, low)


def match_table(doc_blocks, land_ids):
    eq = doc_blocks[None, :, :, None] == land_ids[:, None, None, :]
    has = jnp.any(eq, axis=2)
    first = jnp.argmax(eq, axis=2).astype(jnp.int32)
    return jnp.where(has, first, ACTIVE).astype(jnp.int32).reshape(-1)


def forward_kernel(slot_ref, doc_ref, dn_ref, land_ref,
                   high_ref, low_ref, fit_ref, aligned_ref):
    step = pl.program_id(0)
    doc_count = dn_ref.shape[0] // DOC_BLOCK

    @pl.when(step == 0)
    def _():
        fit_ref[...] = jnp.zeros_like(fit_ref)

    for d in range(doc_count):
        for b in range(LAND_ACTIVE):
            a = slot_ref[(step * doc_count + d) * LAND_ACTIVE + b]
            aligned_ref[d * DOC_BLOCK:(d + 1) * DOC_BLOCK, b * TERM_BLOCK:(b + 1) * TERM_BLOCK] = (
                doc_ref[d * (ACTIVE + 1) + a])
    width = ACTIVE * TERM_BLOCK
    tile = land_ref[:width, :]
    squares = tile.astype(jnp.float32)
    land_norm = lax.rsqrt(jnp.sum(squares * squares, axis=0, keepdims=True) + 1e-06)
    inner = jnp.dot(aligned_ref[...], tile, preferred_element_type=jnp.float32)
    kern = jnp.exp(inner * dn_ref[...] * land_norm - 2.0 * sharpness)
    high = kern.astype(jnp.bfloat16)
    low = (kern - high.astype(jnp.float32)).astype(jnp.bfloat16)
    high_ref[0] = high
    low_ref[0] = low
    coef = land_ref[width:, :]
    pair = jnp.concatenate([high, low], axis=1)
    coef_pair = jnp.concatenate([coef, coef], axis=1)
    dims = (((1,), (1,)), ((), ()))
    fit_ref[...] += lax.dot_general(pair, coef_pair, dims, preferred_element_type=jnp.float32)


def forward(slots, doc_tiles, doc_norm, land_rows, targets):
    doc_rows = doc_norm.shape[0]
    row_height = ACTIVE * TERM_BLOCK + targets
    block_count = land_rows.shape[0] // row_height
    land_count = block_count * LM_BLOCK
    width = ACTIVE * TERM_BLOCK
    grid_spec = pltpu.PrefetchScalarGridSpec(
        num_scalar_prefetch=1,
        grid=(block_count,),
        in_specs=[
            pl.BlockSpec(doc_tiles.shape, lambda l, s: (0, 0, 0)),
            pl.BlockSpec((doc_rows, 1), lambda l, s: (0, 0)),
            pl.BlockSpec((row_height, LM_BLOCK), lambda l, s: (l, 0)),
        ],
        out_specs=[
            pl.BlockSpec((1, doc_rows, LM_BLOCK), lambda l, s: (l, 0, 0)),
            pl.BlockSpec((1, doc_rows, LM_BLOCK), lambda l, s: (l, 0, 0)),
            pl.BlockSpec((doc_rows, targets), lambda l, s: (0, 0)),
        ],
        scratch_shapes=[pltpu.VMEM((doc_rows, width), jnp.bfloat16)],
    )
    return pl.pallas_call(
        forward_kernel,
        grid_spec=grid_spec,
        out_shape=[
            jax.ShapeDtypeStruct((block_count, doc_rows, LM_BLOCK), jnp.bfloat16),
            jax.ShapeDtypeStruct((block_count, doc_rows, LM_BLOCK), jnp.bfloat16),
            jax.ShapeDtypeStruct((doc_rows, targets), jnp.float32),
        ],
        compiler_params=pltpu.CompilerParams(
            dimension_semantics=("arbitrary",), vmem_limit_bytes=48 * 1024 * 1024),
    )(slots, doc_tiles, doc_norm, land_rows)


def sum_over(values, axis, count):
    pieces = values.reshape((count, values.shape[0] // count) + values.shape[1:])
    pieces = lax.all_to_all(pieces, axis, 0, 0, tiled=False)
    return jnp.sum(pieces, axis=0)


def all_sum(values, axis, count):
    mine = sum_over(values, axis, count)
    spread = jnp.broadcast_to(mine[None], (count,) + mine.shape)
    return lax.all_to_all(spread, axis, 0, 0, tiled=False).reshape(values.shape)


def on_device(doc_values, doc_blocks, land_values, land_blocks, coefficients):
    dp_count = lax.axis_size("dp")
    land_count = lax.axis_size("land")
    doc_rows = doc_values.shape[0]
    targets = coefficients.shape[1]
    total_docs = doc_rows * dp_count
    own_blocks = land_values.shape[0] // LM_BLOCK
    doc_count = doc_rows // DOC_BLOCK
    doc_norm = lax.rsqrt(jnp.sum(jnp.square(doc_values.astype(jnp.float32)), axis=1) + 1e-06)
    table = land_blocks.reshape(dp_count, land_count, own_blocks, LAND_ACTIVE)
    own_table = lax.dynamic_index_in_dim(table, lax.axis_index("land"), axis=1, keepdims=False)
    own_table = own_table.reshape(dp_count * own_blocks, LAND_ACTIVE)
    land_rows = lax.all_gather(
        jnp.concatenate([land_values, coefficients], axis=1).T, "dp", axis=0, tiled=True)
    doc_tiles = doc_values.reshape(doc_count, DOC_BLOCK, ACTIVE, TERM_BLOCK).transpose(0, 2, 1, 3)
    doc_tiles = jnp.pad(doc_tiles, ((0, 0), (0, 1), (0, 0), (0, 0)))
    doc_tiles = doc_tiles.reshape(doc_count * (ACTIVE + 1), DOC_BLOCK, TERM_BLOCK)
    slots = match_table(doc_blocks, own_table)
    tile_high, tile_low, fitted = forward(
        slots, doc_tiles, (2.0 * sharpness) * doc_norm.reshape(doc_rows, 1), land_rows, targets)
    fitted = all_sum(fitted, "land", land_count)
    fitted_high, fitted_low = split_pair(fitted)
    fitted_pair = jnp.concatenate([fitted_high, fitted_low], axis=1)
    summed = jnp.einsum("qnl,nt->qlt", tile_high, fitted_pair, preferred_element_type=jnp.float32)
    summed = summed + jnp.einsum("qnl,nt->qlt", tile_low, fitted_pair, preferred_element_type=jnp.float32)
    summed = (summed[:, :, :targets] + summed[:, :, targets:]).reshape(-1, targets)
    result = sum_over(summed, "dp", dp_count)
    return result / total_docs


def solution(mesh):
    placed = (P("dp", None), P("dp", None), P(("dp", "land"), None), P(), P(("dp", "land"), None))
    return jax.shard_map(
        on_device, mesh=mesh, in_specs=placed, out_specs=P(("dp", "land"), None), check_vma=False
    )
```

```python
import jax
import jax.numpy as jnp
from jax import lax
from jax.experimental import pallas as pl
from jax.experimental.pallas import tpu as pltpu
from jax.sharding import PartitionSpec as P

TERM_BLOCK = 128
ACTIVE = 8
LAND_ACTIVE = 8
DOC_BLOCK = 128
LM_BLOCK = 128


sharpness = 2.0


def split_pair(values):
    high = lax.optimization_barrier(values.astype(jnp.bfloat16))
    low = (values - high.astype(jnp.float32)).astype(jnp.bfloat16)
    return (high, low)


def match_table(doc_blocks, land_ids):
    eq = doc_blocks[None, :, :, None] == land_ids[:, None, None, :]
    has = jnp.any(eq, axis=2)
    first = jnp.argmax(eq, axis=2).astype(jnp.int32)
    return jnp.where(has, first, ACTIVE).astype(jnp.int32).reshape(-1)


def forward_kernel(slot_ref, doc_ref, dn_ref, land_ref,
                   tile_ref, fit_ref, aligned_ref):
    step = pl.program_id(0)
    doc_count = dn_ref.shape[0] // DOC_BLOCK

    @pl.when(step == 0)
    def _():
        fit_ref[...] = jnp.zeros_like(fit_ref)

    for d in range(doc_count):
        for b in range(LAND_ACTIVE):
            a = slot_ref[(step * doc_count + d) * LAND_ACTIVE + b]
            aligned_ref[d * DOC_BLOCK:(d + 1) * DOC_BLOCK, b * TERM_BLOCK:(b + 1) * TERM_BLOCK] = (
                doc_ref[d * (ACTIVE + 1) + a])
    width = ACTIVE * TERM_BLOCK
    tile = land_ref[:width, :]
    squares = tile.astype(jnp.float32)
    land_norm = lax.rsqrt(jnp.sum(squares * squares, axis=0, keepdims=True) + 1e-06)
    inner = jnp.dot(aligned_ref[...], tile, preferred_element_type=jnp.float32)
    kern = jnp.exp(inner * dn_ref[...] * land_norm - 2.0 * sharpness)
    high = kern.astype(jnp.bfloat16)
    low = (kern - high.astype(jnp.float32)).astype(jnp.bfloat16)
    tile_ref[0, 0] = high
    tile_ref[0, 1] = low
    coef = land_ref[width:, :]
    pair = jnp.concatenate([high, low], axis=1)
    coef_pair = jnp.concatenate([coef, coef], axis=1)
    dims = (((1,), (1,)), ((), ()))
    fit_ref[...] += lax.dot_general(pair, coef_pair, dims, preferred_element_type=jnp.float32)


def forward(slots, doc_tiles, doc_norm, land_rows, targets):
    doc_rows = doc_norm.shape[0]
    row_height = ACTIVE * TERM_BLOCK + targets
    block_count = land_rows.shape[0] // row_height
    land_count = block_count * LM_BLOCK
    width = ACTIVE * TERM_BLOCK
    grid_spec = pltpu.PrefetchScalarGridSpec(
        num_scalar_prefetch=1,
        grid=(block_count,),
        in_specs=[
            pl.BlockSpec(doc_tiles.shape, lambda l, s: (0, 0, 0)),
            pl.BlockSpec((doc_rows, 1), lambda l, s: (0, 0)),
            pl.BlockSpec((row_height, LM_BLOCK), lambda l, s: (l, 0)),
        ],
        out_specs=[
            pl.BlockSpec((1, 2, doc_rows, LM_BLOCK), lambda l, s: (l, 0, 0, 0)),
            pl.BlockSpec((doc_rows, targets), lambda l, s: (0, 0)),
        ],
        scratch_shapes=[pltpu.VMEM((doc_rows, width), jnp.bfloat16)],
    )
    return pl.pallas_call(
        forward_kernel,
        grid_spec=grid_spec,
        out_shape=[
            jax.ShapeDtypeStruct((block_count, 2, doc_rows, LM_BLOCK), jnp.bfloat16),
            jax.ShapeDtypeStruct((doc_rows, targets), jnp.float32),
        ],
        compiler_params=pltpu.CompilerParams(
            dimension_semantics=("arbitrary",), vmem_limit_bytes=48 * 1024 * 1024),
    )(slots, doc_tiles, doc_norm, land_rows)


def sum_over(values, axis, count):
    pieces = values.reshape((count, values.shape[0] // count) + values.shape[1:])
    pieces = lax.all_to_all(pieces, axis, 0, 0, tiled=False)
    return jnp.sum(pieces, axis=0)


def all_sum(values, axis, count):
    mine = sum_over(values, axis, count)
    spread = jnp.broadcast_to(mine[None], (count,) + mine.shape)
    return lax.all_to_all(spread, axis, 0, 0, tiled=False).reshape(values.shape)


def on_device(doc_values, doc_blocks, land_values, land_blocks, coefficients):
    dp_count = lax.axis_size("dp")
    land_count = lax.axis_size("land")
    doc_rows = doc_values.shape[0]
    targets = coefficients.shape[1]
    total_docs = doc_rows * dp_count
    own_blocks = land_values.shape[0] // LM_BLOCK
    doc_count = doc_rows // DOC_BLOCK
    doc_norm = lax.rsqrt(jnp.sum(jnp.square(doc_values.astype(jnp.float32)), axis=1) + 1e-06)
    table = land_blocks.reshape(dp_count, land_count, own_blocks, LAND_ACTIVE)
    own_table = lax.dynamic_index_in_dim(table, lax.axis_index("land"), axis=1, keepdims=False)
    own_table = own_table.reshape(dp_count * own_blocks, LAND_ACTIVE)
    land_rows = lax.all_gather(
        jnp.concatenate([land_values, coefficients], axis=1).T, "dp", axis=0, tiled=True)
    doc_tiles = doc_values.reshape(doc_count, DOC_BLOCK, ACTIVE, TERM_BLOCK).transpose(0, 2, 1, 3)
    doc_tiles = jnp.pad(doc_tiles, ((0, 0), (0, 1), (0, 0), (0, 0)))
    doc_tiles = doc_tiles.reshape(doc_count * (ACTIVE + 1), DOC_BLOCK, TERM_BLOCK)
    slots = match_table(doc_blocks, own_table)
    tiles, fitted = forward(
        slots, doc_tiles, (2.0 * sharpness) * doc_norm.reshape(doc_rows, 1), land_rows, targets)
    fitted = all_sum(fitted, "land", land_count)
    fitted_high, fitted_low = split_pair(fitted)
    fitted_pair = jnp.concatenate([fitted_high, fitted_low], axis=1)
    pairs = jnp.stack([fitted_pair, fitted_pair])
    summed = jnp.einsum("qsnl,snt->qlt", tiles, pairs, preferred_element_type=jnp.float32)
    summed = (summed[:, :, :targets] + summed[:, :, targets:]).reshape(-1, targets)
    result = sum_over(summed, "dp", dp_count)
    return result / total_docs


def solution(mesh):
    placed = (P("dp", None), P("dp", None), P(("dp", "land"), None), P(), P(("dp", "land"), None))
    return jax.shard_map(
        on_device, mesh=mesh, in_specs=placed, out_specs=P(("dp", "land"), None), check_vma=False
    )
```

```python
import jax
import jax.numpy as jnp
from jax import lax
from jax.experimental import pallas as pl
from jax.experimental.pallas import tpu as pltpu
from jax.sharding import PartitionSpec as P

TERM_BLOCK = 128
ACTIVE = 8
LAND_ACTIVE = 8
DOC_BLOCK = 128
LM_BLOCK = 128


sharpness = 2.0


def split_pair(values):
    high = lax.optimization_barrier(values.astype(jnp.bfloat16))
    low = (values - high.astype(jnp.float32)).astype(jnp.bfloat16)
    return (high, low)


def match_table(doc_blocks, land_ids):
    eq = doc_blocks[None, :, :, None] == land_ids[:, None, None, :]
    has = jnp.any(eq, axis=2)
    first = jnp.argmax(eq, axis=2).astype(jnp.int32)
    return jnp.where(has, first, ACTIVE).astype(jnp.int32).reshape(-1)


def forward_kernel(slot_ref, doc_ref, dn_ref, land_ref,
                   high_ref, low_ref, fit_ref, aligned_ref):
    step = pl.program_id(0)
    doc_count = dn_ref.shape[0] // DOC_BLOCK

    @pl.when(step == 0)
    def _():
        fit_ref[...] = jnp.zeros_like(fit_ref)

    for d in range(doc_count):
        for b in range(LAND_ACTIVE):
            a = slot_ref[(step * doc_count + d) * LAND_ACTIVE + b]
            aligned_ref[d * DOC_BLOCK:(d + 1) * DOC_BLOCK, b * TERM_BLOCK:(b + 1) * TERM_BLOCK] = (
                doc_ref[d * (ACTIVE + 1) + a])
    width = ACTIVE * TERM_BLOCK
    tile = land_ref[:width, :]
    squares = tile.astype(jnp.float32)
    land_norm = lax.rsqrt(jnp.sum(squares * squares, axis=0, keepdims=True) + 1e-06)
    inner = jnp.dot(aligned_ref[...], tile, preferred_element_type=jnp.float32)
    kern = jnp.exp(inner * dn_ref[...] * land_norm - 2.0 * sharpness)
    high = kern.astype(jnp.bfloat16)
    low = (kern - high.astype(jnp.float32)).astype(jnp.bfloat16)
    high_ref[0] = high
    low_ref[0] = low
    coef = land_ref[width:, :]
    pair = jnp.concatenate([high, low], axis=1)
    coef_pair = jnp.concatenate([coef, coef], axis=1)
    coef_pair = jnp.concatenate([coef_pair, jnp.zeros_like(coef_pair)], axis=0)
    dims = (((1,), (1,)), ((), ()))
    fit_ref[...] += lax.dot_general(pair, coef_pair, dims, preferred_element_type=jnp.float32)


def forward(slots, doc_tiles, doc_norm, land_rows, targets):
    doc_rows = doc_norm.shape[0]
    row_height = ACTIVE * TERM_BLOCK + targets
    block_count = land_rows.shape[0] // row_height
    land_count = block_count * LM_BLOCK
    width = ACTIVE * TERM_BLOCK
    grid_spec = pltpu.PrefetchScalarGridSpec(
        num_scalar_prefetch=1,
        grid=(block_count,),
        in_specs=[
            pl.BlockSpec(doc_tiles.shape, lambda l, s: (0, 0, 0)),
            pl.BlockSpec((doc_rows, 1), lambda l, s: (0, 0)),
            pl.BlockSpec((row_height, LM_BLOCK), lambda l, s: (l, 0)),
        ],
        out_specs=[
            pl.BlockSpec((1, doc_rows, LM_BLOCK), lambda l, s: (l, 0, 0)),
            pl.BlockSpec((1, doc_rows, LM_BLOCK), lambda l, s: (l, 0, 0)),
            pl.BlockSpec((doc_rows, 2 * targets), lambda l, s: (0, 0)),
        ],
        scratch_shapes=[pltpu.VMEM((doc_rows, width), jnp.bfloat16)],
    )
    high, low, fitted = pl.pallas_call(
        forward_kernel,
        grid_spec=grid_spec,
        out_shape=[
            jax.ShapeDtypeStruct((block_count, doc_rows, LM_BLOCK), jnp.bfloat16),
            jax.ShapeDtypeStruct((block_count, doc_rows, LM_BLOCK), jnp.bfloat16),
            jax.ShapeDtypeStruct((doc_rows, 2 * targets), jnp.float32),
        ],
        compiler_params=pltpu.CompilerParams(
            dimension_semantics=("arbitrary",), vmem_limit_bytes=48 * 1024 * 1024),
    )(slots, doc_tiles, doc_norm, land_rows)
    return high, low, fitted[:, :targets]


def sum_over(values, axis, count):
    pieces = values.reshape((count, values.shape[0] // count) + values.shape[1:])
    pieces = lax.all_to_all(pieces, axis, 0, 0, tiled=False)
    return jnp.sum(pieces, axis=0)


def all_sum(values, axis, count):
    mine = sum_over(values, axis, count)
    spread = jnp.broadcast_to(mine[None], (count,) + mine.shape)
    return lax.all_to_all(spread, axis, 0, 0, tiled=False).reshape(values.shape)


def on_device(doc_values, doc_blocks, land_values, land_blocks, coefficients):
    dp_count = lax.axis_size("dp")
    land_count = lax.axis_size("land")
    doc_rows = doc_values.shape[0]
    targets = coefficients.shape[1]
    total_docs = doc_rows * dp_count
    own_blocks = land_values.shape[0] // LM_BLOCK
    doc_count = doc_rows // DOC_BLOCK
    doc_norm = lax.rsqrt(jnp.sum(jnp.square(doc_values.astype(jnp.float32)), axis=1) + 1e-06)
    table = land_blocks.reshape(dp_count, land_count, own_blocks, LAND_ACTIVE)
    own_table = lax.dynamic_index_in_dim(table, lax.axis_index("land"), axis=1, keepdims=False)
    own_table = own_table.reshape(dp_count * own_blocks, LAND_ACTIVE)
    land_rows = lax.all_gather(
        jnp.concatenate([land_values, coefficients], axis=1).T, "dp", axis=0, tiled=True)
    doc_tiles = doc_values.reshape(doc_count, DOC_BLOCK, ACTIVE, TERM_BLOCK).transpose(0, 2, 1, 3)
    doc_tiles = jnp.pad(doc_tiles, ((0, 0), (0, 1), (0, 0), (0, 0)))
    doc_tiles = doc_tiles.reshape(doc_count * (ACTIVE + 1), DOC_BLOCK, TERM_BLOCK)
    slots = match_table(doc_blocks, own_table)
    tile_high, tile_low, fitted = forward(
        slots, doc_tiles, (2.0 * sharpness) * doc_norm.reshape(doc_rows, 1), land_rows, targets)
    fitted = all_sum(fitted, "land", land_count)
    fitted_high, fitted_low = split_pair(fitted)
    fitted_pair = jnp.concatenate([fitted_high, fitted_low], axis=1)
    summed = jnp.einsum("qnl,nt->qlt", tile_high, fitted_pair, preferred_element_type=jnp.float32)
    summed = summed + jnp.einsum("qnl,nt->qlt", tile_low, fitted_pair, preferred_element_type=jnp.float32)
    summed = (summed[:, :, :targets] + summed[:, :, targets:]).reshape(-1, targets)
    result = sum_over(summed, "dp", dp_count)
    return result / total_docs


def solution(mesh):
    placed = (P("dp", None), P("dp", None), P(("dp", "land"), None), P(), P(("dp", "land"), None))
    return jax.shard_map(
        on_device, mesh=mesh, in_specs=placed, out_specs=P(("dp", "land"), None), check_vma=False
    )
```

```python
import jax
import jax.numpy as jnp
from jax import lax
from jax.experimental import pallas as pl
from jax.experimental.pallas import tpu as pltpu
from jax.sharding import PartitionSpec as P

TERM_BLOCK = 128
ACTIVE = 8
LAND_ACTIVE = 8
DOC_BLOCK = 128
LM_BLOCK = 128


sharpness = 2.0


def split_pair(values):
    high = lax.optimization_barrier(values.astype(jnp.bfloat16))
    low = (values - high.astype(jnp.float32)).astype(jnp.bfloat16)
    return (high, low)


def match_table(doc_blocks, land_ids):
    eq = doc_blocks[None, :, :, None] == land_ids[:, None, None, :]
    has = jnp.any(eq, axis=2)
    first = jnp.argmax(eq, axis=2).astype(jnp.int32)
    return jnp.where(has, first, ACTIVE).astype(jnp.int32).reshape(-1)


def forward_kernel(slot_ref, block_ref, doc_ref, dn_ref, land_ref,
                   high_ref, low_ref, fit_ref, aligned_ref):
    step = pl.program_id(0)
    doc_count = dn_ref.shape[0] // DOC_BLOCK

    @pl.when(step == 0)
    def _():
        fit_ref[...] = jnp.zeros_like(fit_ref)

    for d in range(doc_count):
        for b in range(LAND_ACTIVE):
            a = slot_ref[(step * doc_count + d) * LAND_ACTIVE + b]
            aligned_ref[d * DOC_BLOCK:(d + 1) * DOC_BLOCK, b * TERM_BLOCK:(b + 1) * TERM_BLOCK] = (
                doc_ref[d * (ACTIVE + 1) + a])
    width = ACTIVE * TERM_BLOCK
    tile = land_ref[:width, :]
    squares = tile.astype(jnp.float32)
    land_norm = lax.rsqrt(jnp.sum(squares * squares, axis=0, keepdims=True) + 1e-06)
    inner = jnp.dot(aligned_ref[...], tile, preferred_element_type=jnp.float32)
    kern = jnp.exp(inner * dn_ref[...] * land_norm - 2.0 * sharpness)
    high = kern.astype(jnp.bfloat16)
    low = (kern - high.astype(jnp.float32)).astype(jnp.bfloat16)
    high_ref[0] = high
    low_ref[0] = low
    coef = land_ref[width:, :]
    pair = jnp.concatenate([high, low], axis=1)
    coef_pair = jnp.concatenate([coef, coef], axis=1)
    dims = (((1,), (1,)), ((), ()))
    fit_ref[...] += lax.dot_general(pair, coef_pair, dims, preferred_element_type=jnp.float32)


def forward(slots, doc_tiles, doc_norm, land_rows, targets, blocks):
    doc_rows = doc_norm.shape[0]
    row_height = ACTIVE * TERM_BLOCK + targets
    block_count = blocks.shape[0]
    land_count = block_count * LM_BLOCK
    width = ACTIVE * TERM_BLOCK
    grid_spec = pltpu.PrefetchScalarGridSpec(
        num_scalar_prefetch=2,
        grid=(block_count,),
        in_specs=[
            pl.BlockSpec(doc_tiles.shape, lambda l, s, k: (0, 0, 0)),
            pl.BlockSpec((doc_rows, 1), lambda l, s, k: (0, 0)),
            pl.BlockSpec((row_height, LM_BLOCK), lambda l, s, k: (k[l], 0)),
        ],
        out_specs=[
            pl.BlockSpec((1, doc_rows, LM_BLOCK), lambda l, s, k: (l, 0, 0)),
            pl.BlockSpec((1, doc_rows, LM_BLOCK), lambda l, s, k: (l, 0, 0)),
            pl.BlockSpec((doc_rows, targets), lambda l, s, k: (0, 0)),
        ],
        scratch_shapes=[pltpu.VMEM((doc_rows, width), jnp.bfloat16)],
    )
    return pl.pallas_call(
        forward_kernel,
        grid_spec=grid_spec,
        out_shape=[
            jax.ShapeDtypeStruct((block_count, doc_rows, LM_BLOCK), jnp.bfloat16),
            jax.ShapeDtypeStruct((block_count, doc_rows, LM_BLOCK), jnp.bfloat16),
            jax.ShapeDtypeStruct((doc_rows, targets), jnp.float32),
        ],
        compiler_params=pltpu.CompilerParams(
            dimension_semantics=("arbitrary",), vmem_limit_bytes=48 * 1024 * 1024),
    )(slots, blocks, doc_tiles, doc_norm, land_rows)


def sum_over(values, axis, count):
    pieces = values.reshape((count, values.shape[0] // count) + values.shape[1:])
    pieces = lax.all_to_all(pieces, axis, 0, 0, tiled=False)
    return jnp.sum(pieces, axis=0)


def all_sum(values, axis, count):
    mine = sum_over(values, axis, count)
    spread = jnp.broadcast_to(mine[None], (count,) + mine.shape)
    return lax.all_to_all(spread, axis, 0, 0, tiled=False).reshape(values.shape)


def on_device(doc_values, doc_blocks, land_values, land_blocks, coefficients):
    dp_count = lax.axis_size("dp")
    land_count = lax.axis_size("land")
    doc_rows = doc_values.shape[0]
    targets = coefficients.shape[1]
    total_docs = doc_rows * dp_count
    own_blocks = land_values.shape[0] // LM_BLOCK
    doc_count = doc_rows // DOC_BLOCK
    doc_norm = lax.rsqrt(jnp.sum(jnp.square(doc_values.astype(jnp.float32)), axis=1) + 1e-06)
    table = land_blocks.reshape(dp_count, land_count, own_blocks, LAND_ACTIVE)
    own_table = lax.dynamic_index_in_dim(table, lax.axis_index("land"), axis=1, keepdims=False)
    own_table = own_table.reshape(dp_count * own_blocks, LAND_ACTIVE)
    own_rows = jnp.concatenate([land_values, coefficients], axis=1).T
    land_rows = lax.all_gather(own_rows, "dp", axis=0, tiled=True)
    own = lax.axis_index("dp")
    rest = jnp.arange(dp_count - 1, dtype=jnp.int32)
    rest = rest + (rest >= own).astype(jnp.int32)
    doc_tiles = doc_values.reshape(doc_count, DOC_BLOCK, ACTIVE, TERM_BLOCK).transpose(0, 2, 1, 3)
    doc_tiles = jnp.pad(doc_tiles, ((0, 0), (0, 1), (0, 0), (0, 0)))
    doc_tiles = doc_tiles.reshape(doc_count * (ACTIVE + 1), DOC_BLOCK, TERM_BLOCK)
    doc_norm = (2.0 * sharpness) * doc_norm.reshape(doc_rows, 1)
    first_high, first_low, fitted_first = forward(
        match_table(doc_blocks, own_table[own][None]), doc_tiles, doc_norm, own_rows, targets,
        jnp.zeros((1,), jnp.int32))
    rest_high, rest_low, fitted = forward(
        match_table(doc_blocks, own_table[rest]), doc_tiles, doc_norm, land_rows, targets, rest)
    fitted = fitted + fitted_first
    fitted = all_sum(fitted, "land", land_count)
    fitted_high, fitted_low = split_pair(fitted)
    fitted_pair = jnp.concatenate([fitted_high, fitted_low], axis=1)
    tile_high = jnp.concatenate([rest_high, first_high], axis=0)
    tile_low = jnp.concatenate([rest_low, first_low], axis=0)
    summed = jnp.einsum("qnl,nt->qlt", tile_high, fitted_pair, preferred_element_type=jnp.float32)
    summed = summed + jnp.einsum("qnl,nt->qlt", tile_low, fitted_pair, preferred_element_type=jnp.float32)
    summed = summed[:, :, :targets] + summed[:, :, targets:]
    index = jnp.arange(dp_count, dtype=jnp.int32)
    order = jnp.where(index == own, dp_count - 1, index - (index > own).astype(jnp.int32))
    summed = summed[order].reshape(-1, targets)
    result = sum_over(summed, "dp", dp_count)
    return result / total_docs


def solution(mesh):
    placed = (P("dp", None), P("dp", None), P(("dp", "land"), None), P(), P(("dp", "land"), None))
    return jax.shard_map(
        on_device, mesh=mesh, in_specs=placed, out_specs=P(("dp", "land"), None), check_vma=False
    )
```

```python
import jax
import jax.numpy as jnp
from jax import lax
from jax.experimental import pallas as pl
from jax.experimental.pallas import tpu as pltpu
from jax.sharding import PartitionSpec as P

TERM_BLOCK = 128
ACTIVE = 8
LAND_ACTIVE = 8
DOC_BLOCK = 128
LM_BLOCK = 128


sharpness = 2.0


def split_pair(values):
    high = lax.optimization_barrier(values.astype(jnp.bfloat16))
    low = (values - high.astype(jnp.float32)).astype(jnp.bfloat16)
    return (high, low)


def match_table(doc_blocks, land_ids):
    eq = doc_blocks[None, :, :, None] == land_ids[:, None, None, :]
    has = jnp.any(eq, axis=2)
    first = jnp.argmax(eq, axis=2).astype(jnp.int32)
    return jnp.where(has, first, ACTIVE).astype(jnp.int32).reshape(-1)


def forward_kernel(slot_ref, block_ref, doc_ref, dn_ref, land_ref,
                   high_ref, low_ref, fit_ref, aligned_ref):
    step = pl.program_id(0)
    doc_count = dn_ref.shape[0] // DOC_BLOCK

    @pl.when(step == 0)
    def _():
        fit_ref[...] = jnp.zeros_like(fit_ref)

    for d in range(doc_count):
        for b in range(LAND_ACTIVE):
            a = slot_ref[(step * doc_count + d) * LAND_ACTIVE + b]
            aligned_ref[d * DOC_BLOCK:(d + 1) * DOC_BLOCK, b * TERM_BLOCK:(b + 1) * TERM_BLOCK] = (
                doc_ref[d * (ACTIVE + 1) + a])
    width = ACTIVE * TERM_BLOCK
    tile = land_ref[:width, :]
    squares = tile.astype(jnp.float32)
    land_norm = lax.rsqrt(jnp.sum(squares * squares, axis=0, keepdims=True) + 1e-06)
    inner = jnp.dot(aligned_ref[...], tile, preferred_element_type=jnp.float32)
    kern = jnp.exp(inner * dn_ref[...] * land_norm - 2.0 * sharpness)
    high = kern.astype(jnp.bfloat16)
    low = (kern - high.astype(jnp.float32)).astype(jnp.bfloat16)
    high_ref[0] = high
    low_ref[0] = low
    coef = land_ref[width:, :]
    pair = jnp.concatenate([high, low], axis=1)
    coef_pair = jnp.concatenate([coef, coef], axis=1)
    dims = (((1,), (1,)), ((), ()))
    fit_ref[...] += lax.dot_general(pair, coef_pair, dims, preferred_element_type=jnp.float32)


def forward(slots, doc_tiles, doc_norm, land_rows, targets, blocks):
    doc_rows = doc_norm.shape[0]
    row_height = ACTIVE * TERM_BLOCK + targets
    block_count = blocks.shape[0]
    land_count = block_count * LM_BLOCK
    width = ACTIVE * TERM_BLOCK
    grid_spec = pltpu.PrefetchScalarGridSpec(
        num_scalar_prefetch=2,
        grid=(block_count,),
        in_specs=[
            pl.BlockSpec(doc_tiles.shape, lambda l, s, k: (0, 0, 0)),
            pl.BlockSpec((doc_rows, 1), lambda l, s, k: (0, 0)),
            pl.BlockSpec((row_height, LM_BLOCK), lambda l, s, k: (k[l], 0)),
        ],
        out_specs=[
            pl.BlockSpec((1, doc_rows, LM_BLOCK), lambda l, s, k: (l, 0, 0)),
            pl.BlockSpec((1, doc_rows, LM_BLOCK), lambda l, s, k: (l, 0, 0)),
            pl.BlockSpec((doc_rows, targets), lambda l, s, k: (0, 0)),
        ],
        scratch_shapes=[pltpu.VMEM((doc_rows, width), jnp.bfloat16)],
    )
    return pl.pallas_call(
        forward_kernel,
        grid_spec=grid_spec,
        out_shape=[
            jax.ShapeDtypeStruct((block_count, doc_rows, LM_BLOCK), jnp.bfloat16),
            jax.ShapeDtypeStruct((block_count, doc_rows, LM_BLOCK), jnp.bfloat16),
            jax.ShapeDtypeStruct((doc_rows, targets), jnp.float32),
        ],
        compiler_params=pltpu.CompilerParams(
            dimension_semantics=("arbitrary",), vmem_limit_bytes=48 * 1024 * 1024),
    )(slots, blocks, doc_tiles, doc_norm, land_rows)


def sum_over(values, axis, count):
    pieces = values.reshape((count, values.shape[0] // count) + values.shape[1:])
    pieces = lax.all_to_all(pieces, axis, 0, 0, tiled=False)
    return jnp.sum(pieces, axis=0)


def all_sum(values, axis, count):
    mine = sum_over(values, axis, count)
    spread = jnp.broadcast_to(mine[None], (count,) + mine.shape)
    return lax.all_to_all(spread, axis, 0, 0, tiled=False).reshape(values.shape)


def on_device(doc_values, doc_blocks, land_values, land_blocks, coefficients):
    dp_count = lax.axis_size("dp")
    land_count = lax.axis_size("land")
    doc_rows = doc_values.shape[0]
    targets = coefficients.shape[1]
    total_docs = doc_rows * dp_count
    own_blocks = land_values.shape[0] // LM_BLOCK
    doc_count = doc_rows // DOC_BLOCK
    doc_norm = lax.rsqrt(jnp.sum(jnp.square(doc_values.astype(jnp.float32)), axis=1) + 1e-06)
    table = land_blocks.reshape(dp_count, land_count, own_blocks, LAND_ACTIVE)
    own_table = lax.dynamic_index_in_dim(table, lax.axis_index("land"), axis=1, keepdims=False)
    own_table = own_table.reshape(dp_count * own_blocks, LAND_ACTIVE)
    own_rows = jnp.concatenate([land_values, coefficients], axis=1).T
    land_rows = lax.all_gather(own_rows, "dp", axis=0, tiled=True)
    own = lax.axis_index("dp")
    partner_rows = lax.ppermute(own_rows, "dp", [(i, i ^ 1) for i in range(dp_count)])
    first_rows = jnp.concatenate([own_rows, partner_rows], axis=0)
    pair_base = own - own % 2
    rest = jnp.arange(dp_count - 2, dtype=jnp.int32)
    rest = rest + 2 * (rest >= pair_base).astype(jnp.int32)
    doc_tiles = doc_values.reshape(doc_count, DOC_BLOCK, ACTIVE, TERM_BLOCK).transpose(0, 2, 1, 3)
    doc_tiles = jnp.pad(doc_tiles, ((0, 0), (0, 1), (0, 0), (0, 0)))
    doc_tiles = doc_tiles.reshape(doc_count * (ACTIVE + 1), DOC_BLOCK, TERM_BLOCK)
    doc_norm = (2.0 * sharpness) * doc_norm.reshape(doc_rows, 1)
    first_high, first_low, fitted_first = forward(
        match_table(doc_blocks, own_table[jnp.stack([own, own ^ 1])]), doc_tiles, doc_norm, first_rows,
        targets, jnp.arange(2, dtype=jnp.int32))
    rest_high, rest_low, fitted = forward(
        match_table(doc_blocks, own_table[rest]), doc_tiles, doc_norm, land_rows, targets, rest)
    fitted = fitted + fitted_first
    fitted = all_sum(fitted, "land", land_count)
    fitted_high, fitted_low = split_pair(fitted)
    fitted_pair = jnp.concatenate([fitted_high, fitted_low], axis=1)
    tile_high = jnp.concatenate([rest_high, first_high], axis=0)
    tile_low = jnp.concatenate([rest_low, first_low], axis=0)
    summed = jnp.einsum("qnl,nt->qlt", tile_high, fitted_pair, preferred_element_type=jnp.float32)
    summed = summed + jnp.einsum("qnl,nt->qlt", tile_low, fitted_pair, preferred_element_type=jnp.float32)
    summed = summed[:, :, :targets] + summed[:, :, targets:]
    index = jnp.arange(dp_count, dtype=jnp.int32)
    order = index - 2 * (index > pair_base + 1).astype(jnp.int32)
    order = jnp.where(index == own, dp_count - 2, order)
    order = jnp.where(index == (own ^ 1), dp_count - 1, order)
    summed = summed[order].reshape(-1, targets)
    result = sum_over(summed, "dp", dp_count)
    return result / total_docs


def solution(mesh):
    placed = (P("dp", None), P("dp", None), P(("dp", "land"), None), P(), P(("dp", "land"), None))
    return jax.shard_map(
        on_device, mesh=mesh, in_specs=placed, out_specs=P(("dp", "land"), None), check_vma=False
    )
```

```python
import jax
import jax.numpy as jnp
from jax import lax
from jax.experimental import pallas as pl
from jax.experimental.pallas import tpu as pltpu
from jax.sharding import PartitionSpec as P

TERM_BLOCK = 128
ACTIVE = 8
LAND_ACTIVE = 8
DOC_BLOCK = 128
LM_BLOCK = 128


sharpness = 2.0


def split_pair(values):
    high = lax.optimization_barrier(values.astype(jnp.bfloat16))
    low = (values - high.astype(jnp.float32)).astype(jnp.bfloat16)
    return (high, low)


def match_table(doc_blocks, land_ids):
    eq = doc_blocks[None, :, :, None] == land_ids[:, None, None, :]
    has = jnp.any(eq, axis=2)
    first = jnp.argmax(eq, axis=2).astype(jnp.int32)
    return jnp.where(has, first, ACTIVE).astype(jnp.int32).reshape(-1)


def forward_kernel(slot_ref, block_ref, doc_ref, dn_ref, land_ref,
                   high_ref, low_ref, fit_ref, aligned_ref):
    step = pl.program_id(0)
    doc_count = dn_ref.shape[0] // DOC_BLOCK

    @pl.when(step == 0)
    def _():
        fit_ref[...] = jnp.zeros_like(fit_ref)

    for d in range(doc_count):
        for b in range(LAND_ACTIVE):
            a = slot_ref[(step * doc_count + d) * LAND_ACTIVE + b]
            aligned_ref[d * DOC_BLOCK:(d + 1) * DOC_BLOCK, b * TERM_BLOCK:(b + 1) * TERM_BLOCK] = (
                doc_ref[d * (ACTIVE + 1) + a])
    width = ACTIVE * TERM_BLOCK
    tile = land_ref[:width, :]
    squares = tile.astype(jnp.float32)
    land_norm = lax.rsqrt(jnp.sum(squares * squares, axis=0, keepdims=True) + 1e-06)
    inner = jnp.dot(aligned_ref[...], tile, preferred_element_type=jnp.float32)
    kern = jnp.exp(inner * dn_ref[...] * land_norm - 2.0 * sharpness)
    high = kern.astype(jnp.bfloat16)
    low = (kern - high.astype(jnp.float32)).astype(jnp.bfloat16)
    high_ref[0] = high
    low_ref[0] = low
    coef = land_ref[width:, :]
    pair = jnp.concatenate([high, low], axis=1)
    coef_pair = jnp.concatenate([coef, coef], axis=1)
    dims = (((1,), (1,)), ((), ()))
    fit_ref[...] += lax.dot_general(pair, coef_pair, dims, preferred_element_type=jnp.float32)


def forward(slots, doc_tiles, doc_norm, land_rows, targets, blocks):
    doc_rows = doc_norm.shape[0]
    row_height = ACTIVE * TERM_BLOCK + targets
    block_count = blocks.shape[0]
    land_count = block_count * LM_BLOCK
    width = ACTIVE * TERM_BLOCK
    grid_spec = pltpu.PrefetchScalarGridSpec(
        num_scalar_prefetch=2,
        grid=(block_count,),
        in_specs=[
            pl.BlockSpec(doc_tiles.shape, lambda l, s, k: (0, 0, 0)),
            pl.BlockSpec((doc_rows, 1), lambda l, s, k: (0, 0)),
            pl.BlockSpec((row_height, LM_BLOCK), lambda l, s, k: (k[l], 0)),
        ],
        out_specs=[
            pl.BlockSpec((1, doc_rows, LM_BLOCK), lambda l, s, k: (l, 0, 0)),
            pl.BlockSpec((1, doc_rows, LM_BLOCK), lambda l, s, k: (l, 0, 0)),
            pl.BlockSpec((doc_rows, targets), lambda l, s, k: (0, 0)),
        ],
        scratch_shapes=[pltpu.VMEM((doc_rows, width), jnp.bfloat16)],
    )
    return pl.pallas_call(
        forward_kernel,
        grid_spec=grid_spec,
        out_shape=[
            jax.ShapeDtypeStruct((block_count, doc_rows, LM_BLOCK), jnp.bfloat16),
            jax.ShapeDtypeStruct((block_count, doc_rows, LM_BLOCK), jnp.bfloat16),
            jax.ShapeDtypeStruct((doc_rows, targets), jnp.float32),
        ],
        compiler_params=pltpu.CompilerParams(
            dimension_semantics=("arbitrary",), vmem_limit_bytes=48 * 1024 * 1024),
    )(slots, blocks, doc_tiles, doc_norm, land_rows)


def sum_over(values, axis, count):
    pieces = values.reshape((count, values.shape[0] // count) + values.shape[1:])
    pieces = lax.all_to_all(pieces, axis, 0, 0, tiled=False)
    return jnp.sum(pieces, axis=0)


def all_sum(values, axis, count):
    mine = sum_over(values, axis, count)
    spread = jnp.broadcast_to(mine[None], (count,) + mine.shape)
    return lax.all_to_all(spread, axis, 0, 0, tiled=False).reshape(values.shape)


def on_device(doc_values, doc_blocks, land_values, land_blocks, coefficients):
    dp_count = lax.axis_size("dp")
    land_count = lax.axis_size("land")
    doc_rows = doc_values.shape[0]
    targets = coefficients.shape[1]
    total_docs = doc_rows * dp_count
    own_blocks = land_values.shape[0] // LM_BLOCK
    doc_count = doc_rows // DOC_BLOCK
    doc_norm = lax.rsqrt(jnp.sum(jnp.square(doc_values.astype(jnp.float32)), axis=1) + 1e-06)
    table = land_blocks.reshape(dp_count, land_count, own_blocks, LAND_ACTIVE)
    own_table = lax.dynamic_index_in_dim(table, lax.axis_index("land"), axis=1, keepdims=False)
    own_table = own_table.reshape(dp_count * own_blocks, LAND_ACTIVE)
    own_rows = jnp.concatenate([land_values, coefficients], axis=1).T
    land_rows = lax.all_gather(own_rows, "dp", axis=0, tiled=True)
    own = lax.axis_index("dp")
    near = 4
    first_rows = jnp.concatenate(
        [own_rows] + [lax.ppermute(own_rows, "dp", [(i, i ^ t) for i in range(dp_count)])
                      for t in range(1, near)], axis=0)
    pair_base = own - own % near
    rest = jnp.arange(dp_count - near, dtype=jnp.int32)
    rest = rest + near * (rest >= pair_base).astype(jnp.int32)
    doc_tiles = doc_values.reshape(doc_count, DOC_BLOCK, ACTIVE, TERM_BLOCK).transpose(0, 2, 1, 3)
    doc_tiles = jnp.pad(doc_tiles, ((0, 0), (0, 1), (0, 0), (0, 0)))
    doc_tiles = doc_tiles.reshape(doc_count * (ACTIVE + 1), DOC_BLOCK, TERM_BLOCK)
    doc_norm = (2.0 * sharpness) * doc_norm.reshape(doc_rows, 1)
    first_high, first_low, fitted_first = forward(
        match_table(doc_blocks, own_table[jnp.stack([own ^ t for t in range(near)])]), doc_tiles,
        doc_norm, first_rows, targets, jnp.arange(near, dtype=jnp.int32))
    rest_high, rest_low, fitted = forward(
        match_table(doc_blocks, own_table[rest]), doc_tiles, doc_norm, land_rows, targets, rest)
    fitted = fitted + fitted_first
    fitted = all_sum(fitted, "land", land_count)
    fitted_high, fitted_low = split_pair(fitted)
    fitted_pair = jnp.concatenate([fitted_high, fitted_low], axis=1)
    tile_high = jnp.concatenate([rest_high, first_high], axis=0)
    tile_low = jnp.concatenate([rest_low, first_low], axis=0)
    summed = jnp.einsum("qnl,nt->qlt", tile_high, fitted_pair, preferred_element_type=jnp.float32)
    summed = summed + jnp.einsum("qnl,nt->qlt", tile_low, fitted_pair, preferred_element_type=jnp.float32)
    summed = summed[:, :, :targets] + summed[:, :, targets:]
    index = jnp.arange(dp_count, dtype=jnp.int32)
    order = index - near * (index >= pair_base + near).astype(jnp.int32)
    group = (index >= pair_base) & (index < pair_base + near)
    order = jnp.where(group, dp_count - near + (index ^ own), order)
    summed = summed[order].reshape(-1, targets)
    result = sum_over(summed, "dp", dp_count)
    return result / total_docs


def solution(mesh):
    placed = (P("dp", None), P("dp", None), P(("dp", "land"), None), P(), P(("dp", "land"), None))
    return jax.shard_map(
        on_device, mesh=mesh, in_specs=placed, out_specs=P(("dp", "land"), None), check_vma=False
    )
```

```python
import jax
import jax.numpy as jnp
from jax import lax
from jax.experimental import pallas as pl
from jax.experimental.pallas import tpu as pltpu
from jax.sharding import PartitionSpec as P

TERM_BLOCK = 128
ACTIVE = 8
LAND_ACTIVE = 8
DOC_BLOCK = 128
LM_BLOCK = 128


sharpness = 2.0


def split_pair(values):
    high = lax.optimization_barrier(values.astype(jnp.bfloat16))
    low = (values - high.astype(jnp.float32)).astype(jnp.bfloat16)
    return (high, low)


def match_table(doc_blocks, land_ids):
    eq = doc_blocks[None, :, :, None] == land_ids[:, None, None, :]
    has = jnp.any(eq, axis=2)
    first = jnp.argmax(eq, axis=2).astype(jnp.int32)
    return jnp.where(has, first, ACTIVE).astype(jnp.int32).reshape(-1)


def forward_kernel(slot_ref, block_ref, doc_ref, dn_ref, land_ref,
                   high_ref, low_ref, fit_ref, aligned_ref):
    step = pl.program_id(0)
    doc_count = dn_ref.shape[0] // DOC_BLOCK

    @pl.when(step == 0)
    def _():
        fit_ref[...] = jnp.zeros_like(fit_ref)

    for d in range(doc_count):
        for b in range(LAND_ACTIVE):
            a = slot_ref[(step * doc_count + d) * LAND_ACTIVE + b]
            aligned_ref[d * DOC_BLOCK:(d + 1) * DOC_BLOCK, b * TERM_BLOCK:(b + 1) * TERM_BLOCK] = (
                doc_ref[d * (ACTIVE + 1) + a])
    width = ACTIVE * TERM_BLOCK
    tile = land_ref[:width, :]
    squares = tile.astype(jnp.float32)
    land_norm = lax.rsqrt(jnp.sum(squares * squares, axis=0, keepdims=True) + 1e-06)
    inner = jnp.dot(aligned_ref[...], tile, preferred_element_type=jnp.float32)
    kern = jnp.exp(inner * dn_ref[...] * land_norm - 2.0 * sharpness)
    high = kern.astype(jnp.bfloat16)
    low = (kern - high.astype(jnp.float32)).astype(jnp.bfloat16)
    high_ref[0] = high
    low_ref[0] = low
    coef = land_ref[width:, :]
    pair = jnp.concatenate([high, low], axis=1)
    coef_pair = jnp.concatenate([coef, coef], axis=1)
    dims = (((1,), (1,)), ((), ()))
    fit_ref[...] += lax.dot_general(pair, coef_pair, dims, preferred_element_type=jnp.float32)


def forward(slots, doc_tiles, doc_norm, land_rows, targets, blocks):
    doc_rows = doc_norm.shape[0]
    row_height = ACTIVE * TERM_BLOCK + targets
    block_count = blocks.shape[0]
    land_count = block_count * LM_BLOCK
    width = ACTIVE * TERM_BLOCK
    grid_spec = pltpu.PrefetchScalarGridSpec(
        num_scalar_prefetch=2,
        grid=(block_count,),
        in_specs=[
            pl.BlockSpec(doc_tiles.shape, lambda l, s, k: (0, 0, 0)),
            pl.BlockSpec((doc_rows, 1), lambda l, s, k: (0, 0)),
            pl.BlockSpec((row_height, LM_BLOCK), lambda l, s, k: (k[l], 0)),
        ],
        out_specs=[
            pl.BlockSpec((1, doc_rows, LM_BLOCK), lambda l, s, k: (l, 0, 0)),
            pl.BlockSpec((1, doc_rows, LM_BLOCK), lambda l, s, k: (l, 0, 0)),
            pl.BlockSpec((doc_rows, targets), lambda l, s, k: (0, 0)),
        ],
        scratch_shapes=[pltpu.VMEM((doc_rows, width), jnp.bfloat16)],
    )
    return pl.pallas_call(
        forward_kernel,
        grid_spec=grid_spec,
        out_shape=[
            jax.ShapeDtypeStruct((block_count, doc_rows, LM_BLOCK), jnp.bfloat16),
            jax.ShapeDtypeStruct((block_count, doc_rows, LM_BLOCK), jnp.bfloat16),
            jax.ShapeDtypeStruct((doc_rows, targets), jnp.float32),
        ],
        compiler_params=pltpu.CompilerParams(
            dimension_semantics=("arbitrary",), vmem_limit_bytes=48 * 1024 * 1024),
    )(slots, blocks, doc_tiles, doc_norm, land_rows)


def sum_over(values, axis, count):
    pieces = values.reshape((count, values.shape[0] // count) + values.shape[1:])
    pieces = lax.all_to_all(pieces, axis, 0, 0, tiled=False)
    return jnp.sum(pieces, axis=0)


def all_sum(values, axis, count):
    mine = sum_over(values, axis, count)
    spread = jnp.broadcast_to(mine[None], (count,) + mine.shape)
    return lax.all_to_all(spread, axis, 0, 0, tiled=False).reshape(values.shape)


def on_device(doc_values, doc_blocks, land_values, land_blocks, coefficients):
    dp_count = lax.axis_size("dp")
    land_count = lax.axis_size("land")
    doc_rows = doc_values.shape[0]
    targets = coefficients.shape[1]
    total_docs = doc_rows * dp_count
    own_blocks = land_values.shape[0] // LM_BLOCK
    doc_count = doc_rows // DOC_BLOCK
    doc_norm = lax.rsqrt(jnp.sum(jnp.square(doc_values.astype(jnp.float32)), axis=1) + 1e-06)
    table = land_blocks.reshape(dp_count, land_count, own_blocks, LAND_ACTIVE)
    own_table = lax.dynamic_index_in_dim(table, lax.axis_index("land"), axis=1, keepdims=False)
    own_table = own_table.reshape(dp_count * own_blocks, LAND_ACTIVE)
    own_rows = jnp.concatenate([land_values, coefficients], axis=1).T
    land_rows = lax.all_gather(own_rows, "dp", axis=0, tiled=True)
    own = lax.axis_index("dp")
    near = 8
    first_rows = jnp.concatenate(
        [own_rows] + [lax.ppermute(own_rows, "dp", [(i, i ^ t) for i in range(dp_count)])
                      for t in range(1, near)], axis=0)
    pair_base = own - own % near
    rest = jnp.arange(dp_count - near, dtype=jnp.int32)
    rest = rest + near * (rest >= pair_base).astype(jnp.int32)
    doc_tiles = doc_values.reshape(doc_count, DOC_BLOCK, ACTIVE, TERM_BLOCK).transpose(0, 2, 1, 3)
    doc_tiles = jnp.pad(doc_tiles, ((0, 0), (0, 1), (0, 0), (0, 0)))
    doc_tiles = doc_tiles.reshape(doc_count * (ACTIVE + 1), DOC_BLOCK, TERM_BLOCK)
    doc_norm = (2.0 * sharpness) * doc_norm.reshape(doc_rows, 1)
    first_high, first_low, fitted_first = forward(
        match_table(doc_blocks, own_table[jnp.stack([own ^ t for t in range(near)])]), doc_tiles,
        doc_norm, first_rows, targets, jnp.arange(near, dtype=jnp.int32))
    rest_high, rest_low, fitted = forward(
        match_table(doc_blocks, own_table[rest]), doc_tiles, doc_norm, land_rows, targets, rest)
    fitted = fitted + fitted_first
    fitted = all_sum(fitted, "land", land_count)
    fitted_high, fitted_low = split_pair(fitted)
    fitted_pair = jnp.concatenate([fitted_high, fitted_low], axis=1)
    tile_high = jnp.concatenate([rest_high, first_high], axis=0)
    tile_low = jnp.concatenate([rest_low, first_low], axis=0)
    summed = jnp.einsum("qnl,nt->qlt", tile_high, fitted_pair, preferred_element_type=jnp.float32)
    summed = summed + jnp.einsum("qnl,nt->qlt", tile_low, fitted_pair, preferred_element_type=jnp.float32)
    summed = summed[:, :, :targets] + summed[:, :, targets:]
    index = jnp.arange(dp_count, dtype=jnp.int32)
    order = index - near * (index >= pair_base + near).astype(jnp.int32)
    group = (index >= pair_base) & (index < pair_base + near)
    order = jnp.where(group, dp_count - near + (index ^ own), order)
    summed = summed[order].reshape(-1, targets)
    result = sum_over(summed, "dp", dp_count)
    return result / total_docs


def solution(mesh):
    placed = (P("dp", None), P("dp", None), P(("dp", "land"), None), P(), P(("dp", "land"), None))
    return jax.shard_map(
        on_device, mesh=mesh, in_specs=placed, out_specs=P(("dp", "land"), None), check_vma=False
    )
```

```python
import jax
import jax.numpy as jnp
from jax import lax
from jax.experimental import pallas as pl
from jax.experimental.pallas import tpu as pltpu
from jax.sharding import PartitionSpec as P

TERM_BLOCK = 128
ACTIVE = 8
LAND_ACTIVE = 8
DOC_BLOCK = 128
LM_BLOCK = 128


sharpness = 2.0


def split_pair(values):
    high = lax.optimization_barrier(values.astype(jnp.bfloat16))
    low = (values - high.astype(jnp.float32)).astype(jnp.bfloat16)
    return (high, low)


def match_table(doc_blocks, land_ids):
    eq = doc_blocks[None, :, :, None] == land_ids[:, None, None, :]
    has = jnp.any(eq, axis=2)
    first = jnp.argmax(eq, axis=2).astype(jnp.int32)
    return jnp.where(has, first, ACTIVE).astype(jnp.int32).reshape(-1)


def forward_kernel(slot_ref, block_ref, doc_ref, dn_ref, land_ref,
                   high_ref, low_ref, fit_ref, aligned_ref):
    step = pl.program_id(0)
    doc_count = dn_ref.shape[0] // DOC_BLOCK

    @pl.when(step == 0)
    def _():
        fit_ref[...] = jnp.zeros_like(fit_ref)

    for d in range(doc_count):
        for b in range(LAND_ACTIVE):
            a = slot_ref[(step * doc_count + d) * LAND_ACTIVE + b]
            aligned_ref[d * DOC_BLOCK:(d + 1) * DOC_BLOCK, b * TERM_BLOCK:(b + 1) * TERM_BLOCK] = (
                doc_ref[d * (ACTIVE + 1) + a])
    width = ACTIVE * TERM_BLOCK
    tile = land_ref[:width, :]
    squares = tile.astype(jnp.float32)
    land_norm = lax.rsqrt(jnp.sum(squares * squares, axis=0, keepdims=True) + 1e-06)
    inner = jnp.dot(aligned_ref[...], tile, preferred_element_type=jnp.float32)
    kern = jnp.exp(inner * dn_ref[...] * land_norm - 2.0 * sharpness)
    high = kern.astype(jnp.bfloat16)
    low = (kern - high.astype(jnp.float32)).astype(jnp.bfloat16)
    high_ref[0] = high
    low_ref[0] = low
    coef = land_ref[width:, :]
    pair = jnp.concatenate([high, low], axis=1)
    coef_pair = jnp.concatenate([coef, coef], axis=1)
    dims = (((1,), (1,)), ((), ()))
    fit_ref[...] += lax.dot_general(pair, coef_pair, dims, preferred_element_type=jnp.float32)


def forward(slots, doc_tiles, doc_norm, land_rows, targets, blocks):
    doc_rows = doc_norm.shape[0]
    row_height = ACTIVE * TERM_BLOCK + targets
    block_count = blocks.shape[0]
    land_count = block_count * LM_BLOCK
    width = ACTIVE * TERM_BLOCK
    grid_spec = pltpu.PrefetchScalarGridSpec(
        num_scalar_prefetch=2,
        grid=(block_count,),
        in_specs=[
            pl.BlockSpec(doc_tiles.shape, lambda l, s, k: (0, 0, 0)),
            pl.BlockSpec((doc_rows, 1), lambda l, s, k: (0, 0)),
            pl.BlockSpec((row_height, LM_BLOCK), lambda l, s, k: (k[l], 0)),
        ],
        out_specs=[
            pl.BlockSpec((1, doc_rows, LM_BLOCK), lambda l, s, k: (l, 0, 0)),
            pl.BlockSpec((1, doc_rows, LM_BLOCK), lambda l, s, k: (l, 0, 0)),
            pl.BlockSpec((doc_rows, targets), lambda l, s, k: (0, 0)),
        ],
        scratch_shapes=[pltpu.VMEM((doc_rows, width), jnp.bfloat16)],
    )
    return pl.pallas_call(
        forward_kernel,
        grid_spec=grid_spec,
        out_shape=[
            jax.ShapeDtypeStruct((block_count, doc_rows, LM_BLOCK), jnp.bfloat16),
            jax.ShapeDtypeStruct((block_count, doc_rows, LM_BLOCK), jnp.bfloat16),
            jax.ShapeDtypeStruct((doc_rows, targets), jnp.float32),
        ],
        compiler_params=pltpu.CompilerParams(
            dimension_semantics=("arbitrary",), vmem_limit_bytes=48 * 1024 * 1024),
    )(slots, blocks, doc_tiles, doc_norm, land_rows)


def sum_over(values, axis, count):
    pieces = values.reshape((count, values.shape[0] // count) + values.shape[1:])
    pieces = lax.all_to_all(pieces, axis, 0, 0, tiled=False)
    return jnp.sum(pieces, axis=0)


def all_sum(values, axis, count):
    mine = sum_over(values, axis, count)
    spread = jnp.broadcast_to(mine[None], (count,) + mine.shape)
    return lax.all_to_all(spread, axis, 0, 0, tiled=False).reshape(values.shape)


def on_device(doc_values, doc_blocks, land_values, land_blocks, coefficients):
    dp_count = lax.axis_size("dp")
    land_count = lax.axis_size("land")
    doc_rows = doc_values.shape[0]
    targets = coefficients.shape[1]
    total_docs = doc_rows * dp_count
    own_blocks = land_values.shape[0] // LM_BLOCK
    doc_count = doc_rows // DOC_BLOCK
    doc_norm = lax.rsqrt(jnp.sum(jnp.square(doc_values.astype(jnp.float32)), axis=1) + 1e-06)
    table = land_blocks.reshape(dp_count, land_count, own_blocks, LAND_ACTIVE)
    own_table = lax.dynamic_index_in_dim(table, lax.axis_index("land"), axis=1, keepdims=False)
    own_table = own_table.reshape(dp_count * own_blocks, LAND_ACTIVE)
    own_rows = jnp.concatenate([land_values, coefficients], axis=1).T
    land_rows = lax.all_gather(own_rows, "dp", axis=0, tiled=True)
    own = lax.axis_index("dp")
    near = 4
    first_rows = jnp.concatenate(
        [own_rows] + [lax.ppermute(own_rows, "dp", [(i, i ^ t) for i in range(dp_count)])
                      for t in range(1, near)], axis=0)
    pair_base = own - own % near
    rest = jnp.arange(dp_count - near, dtype=jnp.int32)
    rest = rest + near * (rest >= pair_base).astype(jnp.int32)
    doc_tiles = doc_values.reshape(doc_count, DOC_BLOCK, ACTIVE, TERM_BLOCK).transpose(0, 2, 1, 3)
    doc_tiles = jnp.pad(doc_tiles, ((0, 0), (0, 1), (0, 0), (0, 0)))
    doc_tiles = doc_tiles.reshape(doc_count * (ACTIVE + 1), DOC_BLOCK, TERM_BLOCK)
    doc_norm = (2.0 * sharpness) * doc_norm.reshape(doc_rows, 1)
    first_high, first_low, fitted_first = forward(
        match_table(doc_blocks, own_table[jnp.stack([own ^ t for t in range(near)])]), doc_tiles,
        doc_norm, first_rows, targets, jnp.arange(near, dtype=jnp.int32))
    rest_high, rest_low, fitted = forward(
        match_table(doc_blocks, own_table[rest]), doc_tiles, doc_norm, land_rows, targets, rest)
    fitted = fitted + fitted_first
    fitted = all_sum(fitted, "land", land_count)
    fitted_high, fitted_low = split_pair(fitted)
    fitted_pair = jnp.concatenate([fitted_high, fitted_low], axis=1)
    parts = []
    for tile_high, tile_low in ((rest_high, rest_low), (first_high, first_low)):
        part = jnp.einsum("qnl,nt->qlt", tile_high, fitted_pair, preferred_element_type=jnp.float32)
        part = part + jnp.einsum("qnl,nt->qlt", tile_low, fitted_pair, preferred_element_type=jnp.float32)
        parts.append(part[:, :, :targets] + part[:, :, targets:])
    summed = jnp.concatenate(parts, axis=0)
    index = jnp.arange(dp_count, dtype=jnp.int32)
    order = index - near * (index >= pair_base + near).astype(jnp.int32)
    group = (index >= pair_base) & (index < pair_base + near)
    order = jnp.where(group, dp_count - near + (index ^ own), order)
    summed = summed[order].reshape(-1, targets)
    result = sum_over(summed, "dp", dp_count)
    return result / total_docs


def solution(mesh):
    placed = (P("dp", None), P("dp", None), P(("dp", "land"), None), P(), P(("dp", "land"), None))
    return jax.shard_map(
        on_device, mesh=mesh, in_specs=placed, out_specs=P(("dp", "land"), None), check_vma=False
    )
```
